256 devices in a mesh: expert: 8 (over x, core), tensor: 32 (over z, y).
Axes of the slice: x: 4, y: 4, z: 8, core: 2. Of those that a mesh axis runs over, the one named last changes fastest.
Arguments:
- resid: bfloat16 [16384, 2048], P(('expert', 'tensor')), may hold values from -6 to 6
- contexts: bfloat16 [16384, 4096], P('expert', 'tensor'), may hold values from -6 to 6
- att_routes: int32 [16384, 2], P('expert'), may hold values from 0 to 7, all different within a row
- att_scores: float32 [16384, 2], P('expert'), may hold values from -6 to 6
- att_out_w: bfloat16 [8, 2048, 2048], P(None, 'tensor'), may hold values from -0.125 to 0.125
- norm_gain: bfloat16 [2048], replicated, may hold values from 0.25 to 1.75
- router_w: bfloat16 [2048, 8], replicated, may hold values from -0.125 to 0.125
- mlp_routes: int32 [16384, 2], P(('expert', 'tensor')), may hold values from 0 to 7, all different within a row
- split_rule: int32 [16384, 2], P(('expert', 'tensor')), may hold values from 0 to 2519
- placement: int32 [32], replicated, may hold values from 0 to 7, as said below
- cap_blocks: int32 [32], replicated, may hold values from 1 to 2, as said below
- w_gate_up: bfloat16 [32, 2048, 2, 5632], P('tensor', None, None, 'expert'), as said below
- w_down: bfloat16 [32, 5632, 2048], P('tensor', 'expert'), as said below
- final_gain: bfloat16 [2048], replicated, may hold values from 0.25 to 1.75
Outputs:
- stream_out: bfloat16 [16384, 2048], P(('expert', 'tensor'))
- normalized: bfloat16 [16384, 2048], P(('expert', 'tensor'))
The draws below stay inside these ranges and needn't reach their ends.
Inputs may be any that keep to these rules, and one draw needn't show every extreme that they name: `att_routes`: each row names 2 different experts. `mlp_routes`: each row names 2 different experts. `placement`: every expert is held by at least one slot. `cap_blocks`: some slot accepts 2 blocks. `w_gate_up`: slots that hold the same expert hold equal weights. `w_down`: slots that hold the same expert hold equal weights.
All inputs are finite; a program needn't handle non-finite values.
Results may differ from the reference program's by a relative error of at most 0.023.
Values may be sent and summed in bfloat16 or wider, within the bound.
No kernel may reach another device: no remote copies, remote signals or barrier semaphores. Data moves between devices by JAX's collectives and lax.ppermute only.
A program may use at most 64 MiB of HBM per device.

```python
import jax
import jax.numpy as jnp
from jax import lax

D = 2048
CTX = 2048
FF = 5632
E_ATT = 8
E_MLP = 8
TOP = 2
MAXB = 2
ROWS = 64
REPLICAS = 32
SOURCES = 256
TOKENS = 16384
CTXS = 64
BLOCK = 2
CAPM = 4
N_EXPERT = 8
N_TENSOR = 32


def replica_table(key):
    base_key = jax.random.fold_in(key, 101)
    extra = jax.random.randint(jax.random.fold_in(base_key, 1), (REPLICAS - E_MLP,), 0, E_MLP).astype(jnp.int32)
    listed = jnp.concatenate([jnp.arange(E_MLP, dtype=jnp.int32), extra])
    order = jax.random.permutation(jax.random.fold_in(base_key, 2), REPLICAS)
    return listed[order].astype(jnp.int32)


def expert_normal(key, salt, expert_id, shape):
    return jax.random.normal(jax.random.fold_in(jax.random.fold_in(key, salt), expert_id), shape, jnp.float32)


def draw_placement(key, part):
    return replica_table(key)


def draw_w_gate_up(key, part):
    listed = replica_table(key)
    values = jax.vmap(lambda expert_id: expert_normal(key, 202, expert_id, (D, 2, FF)))(listed)
    return (values * D ** (-0.5)).astype(jnp.bfloat16)


def draw_w_down(key, part):
    listed = replica_table(key)
    values = jax.vmap(lambda expert_id: expert_normal(key, 203, expert_id, (FF, D)))(listed)
    return (values * FF ** (-0.5)).astype(jnp.bfloat16)


def draw_cap_blocks(key, part):
    values = jax.random.randint(jax.random.fold_in(key, 303), (REPLICAS,), 1, MAXB + 1)
    chosen_slot = jax.random.randint(jax.random.fold_in(key, 304), (), 0, REPLICAS)
    return jnp.where(jnp.arange(REPLICAS) == chosen_slot, MAXB, values).astype(jnp.int32)


def touch_ends(entries, own_key, low, largest):
    spot = [jax.random.randint(jax.random.fold_in(own_key, axis), (), 0, length) for axis, length in enumerate(entries.shape)]
    main_axis = entries.shape.index(max(entries.shape))
    next_to = spot[:main_axis] + [(spot[main_axis] + 1) % entries.shape[main_axis]] + spot[main_axis + 1:]
    return entries.at[tuple(spot)].set(low).at[tuple(next_to)].set(largest)


def levels(stream_key, dims, pieces, low, largest):
    def one(dim, parts):
        heights = jax.random.uniform(jax.random.fold_in(jax.random.fold_in(stream_key, 6), dim), (parts,), jnp.float32, low / len(pieces), largest / len(pieces))
        return jnp.repeat(jnp.exp(heights), dims[dim] // parts).reshape((-1,) + (1,) * (len(dims) - dim - 1))

    level = one(*pieces[0])
    for cut in pieces[1:]:
        level = level * one(*cut)
    return level


def choose_distinct(stream_key, rows, number_of, top, lift):
    sequence = jax.random.permutation(jax.random.fold_in(stream_key, 1), number_of)
    favour = sequence
    for power in range(3):
        favour = favour * favour // number_of
    favour = favour * lift // number_of
    chance = jax.random.randint(jax.random.fold_in(stream_key, 2), (rows, number_of), 0, 4096) + favour
    sure = jax.random.permutation(jax.random.fold_in(stream_key, 3), rows)[jnp.arange(number_of) % rows]
    chance = jnp.where(jnp.arange(rows)[:, None] == sure[None, :], 1 << 14, chance)
    merit = chance * number_of + jnp.arange(number_of)
    return lax.top_k(merit.astype(jnp.int32), top)[1].astype(jnp.int32)


def gaussian(stream_key, extent, deviation, limit, cuts=(), kind=jnp.bfloat16):
    level = levels(stream_key, extent, cuts, -0.22, 0.18) if cuts else 1.0
    result = jax.random.normal(stream_key, extent, jnp.float32) * deviation * level
    return jnp.minimum(jnp.maximum(result, -limit), limit).astype(kind)


def setup_inputs(seed: int = 0) -> dict:
    key_list = jax.random.split(jax.random.key(seed), 15)
    resid = gaussian(key_list[0], (TOKENS, D), 1.0, 6.0, ((0, 256),))
    contexts = gaussian(key_list[1], (TOKENS, CTX * TOP), 1.0, 6.0, ((0, 8), (1, 32)))
    att_routes = choose_distinct(key_list[2], TOKENS, E_ATT, TOP, 2048)
    att_scores = gaussian(key_list[3], (TOKENS, TOP), 1.5, 6.0, ((0, 8),), jnp.float32)
    att_out_w = gaussian(key_list[4], (E_ATT, CTX, D), CTX ** -0.5, 0.125, ((1, 32),))
    norm_gain = jnp.clip(1.0 + 0.15 * jax.random.normal(key_list[5], (D,), jnp.float32), 0.25, 1.75).astype(jnp.bfloat16)
    router_w = gaussian(key_list[6], (D, E_MLP), D ** -0.5, 0.125)
    mlp_routes = choose_distinct(key_list[7], TOKENS, E_MLP, TOP, 4096)
    split_rule = touch_ends(jax.random.randint(key_list[8], (TOKENS, TOP), 0, 2520), jax.random.fold_in(key_list[8], 1), 0, 2519).astype(jnp.int32)
    placement = draw_placement(jax.random.fold_in(key_list[14], 71), 0)
    cap_blocks = draw_cap_blocks(jax.random.fold_in(key_list[14], 71), 0)
    w_gate_up = draw_w_gate_up(jax.random.fold_in(key_list[14], 71), 0)
    w_down = draw_w_down(jax.random.fold_in(key_list[14], 71), 0)
    final_gain = jnp.clip(1.0 + 0.15 * jax.random.normal(key_list[13], (D,), jnp.float32), 0.25, 1.75).astype(jnp.bfloat16)
    return {"resid": resid, "contexts": contexts, "att_routes": att_routes, "att_scores": att_scores, "att_out_w": att_out_w, "norm_gain": norm_gain, "router_w": router_w, "mlp_routes": mlp_routes, "split_rule": split_rule, "placement": placement, "cap_blocks": cap_blocks, "w_gate_up": w_gate_up, "w_down": w_down, "final_gain": final_gain}


norm_eps = 1e-06

def rms_norm(values, gain):
    scale = lax.rsqrt(lax.optimization_barrier(jnp.mean(values * values, axis=-1, keepdims=True)) + norm_eps)
    return values * scale * gain.astype(values.dtype)

def pair_gates(scores):
    first = jax.nn.sigmoid(scores[:, 0] - scores[:, 1])
    return jnp.stack([first, 1.0 - first], axis=1)

def reference(resid, contexts, att_routes, att_scores, att_out_w, norm_gain, router_w, mlp_routes, split_rule, placement, cap_blocks, w_gate_up, w_down, final_gain):
    token_count = resid.shape[0]
    gate_att = pair_gates(att_scores.astype(jnp.float32))
    chosen = (att_routes[:, :, None] == jnp.arange(E_ATT, dtype=jnp.int32)[None, None, :]).astype(jnp.float32)
    weighted = chosen * gate_att[:, :, None]
    context_slices = contexts.reshape(token_count, N_TENSOR, CTXS, TOP)
    out_slices = att_out_w.reshape(E_ATT, N_TENSOR, CTXS, D)

    def attention_step(running, slice_index):
        context_part = lax.dynamic_index_in_dim(context_slices, slice_index, 1, keepdims=False).astype(jnp.float32)
        mixed = jnp.einsum('tke,tck->tec', weighted, context_part).astype(jnp.bfloat16).reshape(token_count, E_ATT * CTXS)
        weight_part = lax.dynamic_index_in_dim(out_slices, slice_index, 1, keepdims=False).reshape(E_ATT * CTXS, D)
        partial_sum = jnp.dot(mixed, weight_part, preferred_element_type=jnp.float32)
        rounded = lax.optimization_barrier(partial_sum.astype(jnp.bfloat16))
        return (running + rounded.astype(jnp.float32), None)
    attention, _ = lax.scan(attention_step, jnp.zeros((token_count, D), jnp.float32), jnp.arange(N_TENSOR, dtype=jnp.int32))
    stream = (resid.astype(jnp.float32) + attention).astype(jnp.bfloat16)
    normed = rms_norm(stream.astype(jnp.float32), norm_gain).astype(jnp.bfloat16)
    logits = jnp.dot(normed, router_w, preferred_element_type=jnp.float32)
    gate_mlp = pair_gates(jnp.take_along_axis(logits, mlp_routes, axis=1))
    slot_ids = jnp.arange(REPLICAS, dtype=jnp.int32)
    expert_ids = jnp.arange(E_MLP, dtype=jnp.int32)
    copies = lax.optimization_barrier(jnp.sum((placement[None, :] == expert_ids[:, None]).astype(jnp.int32), axis=1)).astype(jnp.int32)
    earlier = lax.optimization_barrier(jnp.sum(((placement[None, :] == placement[:, None]) & (slot_ids[None, :] < slot_ids[:, None])).astype(jnp.int32), axis=1)).astype(jnp.int32)
    route_onehot = (mlp_routes[:, :, None] == expert_ids[None, None, :]).astype(jnp.int32)
    route_copies = lax.optimization_barrier(jnp.sum(route_onehot * copies[None, None, :], axis=2)).astype(jnp.int32)
    replica_rank = jnp.remainder(split_rule, route_copies).astype(jnp.int32)
    match = ((placement[None, None, :] == mlp_routes[:, :, None]) & (earlier[None, None, :] == replica_rank[:, :, None])).astype(jnp.int32)
    replica_slot = lax.optimization_barrier(jnp.sum(match * slot_ids[None, None, :], axis=2)).astype(jnp.int32)
    capacity = (lax.optimization_barrier(jnp.sum(match * cap_blocks[None, None, :], axis=2)) * BLOCK).astype(jnp.int32)
    per_source = match.reshape(SOURCES, ROWS * TOP, REPLICAS)
    before = jnp.cumsum(per_source, axis=1) - per_source
    arrival = lax.optimization_barrier(jnp.sum(before * per_source, axis=2)).astype(jnp.int32).reshape(token_count, TOP)
    is_kept = arrival < capacity
    source_index = (jnp.arange(token_count, dtype=jnp.int32) // ROWS)[:, None]
    position = (replica_slot * (SOURCES * CAPM) + source_index * CAPM + arrival).astype(jnp.int32)
    position = jnp.where(is_kept, position, REPLICAS * SOURCES * CAPM).astype(jnp.int32)
    flat_rows = jnp.broadcast_to(normed[:, None, :], (token_count, TOP, D)).reshape(token_count * TOP, D)
    buffer = jnp.zeros((REPLICAS * SOURCES * CAPM, D), jnp.bfloat16).at[position.reshape(-1)].set(flat_rows, mode='drop')
    stacked = buffer.reshape(REPLICAS, SOURCES * CAPM, D)
    unit_slice = FF // N_EXPERT

    def expert_run(replica):
        rows_in = lax.dynamic_index_in_dim(stacked, replica, 0, keepdims=False)
        gate_up = lax.dynamic_index_in_dim(w_gate_up, replica, 0, keepdims=False).reshape(D, 2 * FF)
        both = jnp.dot(rows_in, gate_up, preferred_element_type=jnp.float32)
        hidden = (jax.nn.silu(both[:, :FF]) * both[:, FF:]).astype(jnp.bfloat16)
        hidden_parts = hidden.reshape(SOURCES * CAPM, N_EXPERT, unit_slice)
        down_parts = lax.dynamic_index_in_dim(w_down, replica, 0, keepdims=False).reshape(N_EXPERT, unit_slice, D)

        def part_step(running, slice_index):
            hidden_part = lax.dynamic_index_in_dim(hidden_parts, slice_index, 1, keepdims=False)
            down_part = lax.dynamic_index_in_dim(down_parts, slice_index, 0, keepdims=False)
            rounded = lax.optimization_barrier(jnp.dot(hidden_part, down_part, preferred_element_type=jnp.float32).astype(jnp.bfloat16))
            return (running + rounded.astype(jnp.float32), None)
        summed, _ = lax.scan(part_step, jnp.zeros((SOURCES * CAPM, D), jnp.float32), jnp.arange(N_EXPERT, dtype=jnp.int32))
        return summed.astype(jnp.bfloat16)
    outputs = lax.map(expert_run, jnp.arange(REPLICAS, dtype=jnp.int32))
    flat_out = outputs.reshape(REPLICAS * SOURCES * CAPM, D)
    safe_index = jnp.where(is_kept, position, 0).astype(jnp.int32)
    fetched = flat_out[safe_index.reshape(-1)].reshape(token_count, TOP, D).astype(jnp.float32)
    factors = gate_mlp * is_kept.astype(jnp.float32)
    expert_mix = fetched[:, 0, :] * factors[:, 0:1] + fetched[:, 1, :] * factors[:, 1:2]
    after = stream.astype(jnp.float32) + expert_mix
    return (after.astype(jnp.bfloat16), rms_norm(after, final_gain).astype(jnp.bfloat16))
```

```python
import jax
import jax.numpy as jnp
from jax import lax
from jax.sharding import Mesh, PartitionSpec as P

MAXB = 2
TENSOR = ("tz", "ty")


norm_eps = 1e-06


def rms_norm(values, gain):
    scale = lax.rsqrt(jnp.mean(values * values, axis=-1, keepdims=True) + norm_eps)
    return values * scale * gain.astype(values.dtype)


def pair_gates(scores):
    first = jax.nn.silu(scores[:, 0:1] * 0.0) * 0.0 + jax.nn.sigmoid(
        scores[:, 0:1] - scores[:, 1:2]
    )
    first = first[:, 0]
    return jnp.stack([first, 1.0 - first], axis=1)


def activate(shard_piece, w_gate_up):
    both = jnp.einsum(
        "tsecd,sdgf->tsecgf", shard_piece, w_gate_up, preferred_element_type=jnp.float32
    )
    hidden = (jax.nn.silu(both[:, :, :, :, 0, :]) * both[:, :, :, :, 1, :]).astype(jnp.bfloat16)
    hidden = jnp.transpose(hidden, (0, 2, 3, 1, 4))
    return hidden.reshape(
        hidden.shape[0] * hidden.shape[1] * hidden.shape[2], hidden.shape[3], hidden.shape[4]
    )


def per_device(
    resid,
    contexts,
    att_routes,
    att_scores,
    att_out_w,
    norm_gain,
    router_w,
    mlp_routes,
    split_rule,
    placement,
    cap_blocks,
    w_gate_up,
    w_down,
    final_gain,
):
    n_tensor = lax.axis_size(TENSOR)
    row_count = resid.shape[0]
    model_width = resid.shape[1]
    group_rows = contexts.shape[0]
    att_experts = att_out_w.shape[0]
    slice_ctx = att_out_w.shape[1]
    top_count = att_routes.shape[1]
    gate_att = pair_gates(att_scores)
    chosen = (
        att_routes[:, :, None] == jnp.arange(att_experts, dtype=jnp.int32)[None, None, :]
    ).astype(jnp.float32)
    weighted = chosen * gate_att[:, :, None]
    context_part = contexts.reshape(group_rows, slice_ctx, top_count).astype(jnp.float32)
    mixed = (
        jnp.einsum("tke,tck->tec", weighted, context_part)
        .astype(jnp.bfloat16)
        .reshape(group_rows, att_experts * slice_ctx)
    )
    weight_flat = att_out_w.reshape(att_experts * slice_ctx, model_width)
    row_block = mixed
    partial = jnp.dot(row_block, weight_flat, preferred_element_type=jnp.float32).astype(jnp.bfloat16)
    partial = lax.psum_scatter(partial, "tz", scatter_dimension=0, tiled=True)
    attention = lax.psum_scatter(partial, "ty", scatter_dimension=0, tiled=True).astype(jnp.float32)
    stream = (resid.astype(jnp.float32) + attention).astype(jnp.bfloat16)
    normed = rms_norm(stream.astype(jnp.float32), norm_gain).astype(jnp.bfloat16)
    logits = jnp.dot(normed, router_w, preferred_element_type=jnp.float32)
    gate_mlp = pair_gates(jnp.take_along_axis(logits, mlp_routes, axis=1))
    replicas = placement.shape[0]
    slots = w_gate_up.shape[0]
    expert_total = router_w.shape[1]
    block_rows = max(1, row_count * top_count // (2 * replicas))
    capacity_rows = MAXB * block_rows
    slot_ids = jnp.arange(replicas, dtype=jnp.int32)
    expert_ids = jnp.arange(expert_total, dtype=jnp.int32)
    copies = jnp.sum((placement[None, :] == expert_ids[:, None]).astype(jnp.int32), axis=1)
    earlier = jnp.sum(
        (
            (placement[None, :] == placement[:, None]) & (slot_ids[None, :] < slot_ids[:, None])
        ).astype(jnp.int32),
        axis=1,
    )
    route_onehot = (mlp_routes[:, :, None] == expert_ids[None, None, :]).astype(jnp.int32)
    route_copies = jnp.sum(route_onehot * copies[None, None, :], axis=2)
    replica_rank = jnp.remainder(split_rule, route_copies)
    match = (
        (placement[None, None, :] == mlp_routes[:, :, None])
        & (earlier[None, None, :] == replica_rank[:, :, None])
    ).astype(jnp.int32)
    replica_slot = jnp.sum(match * slot_ids[None, None, :], axis=2)
    capacity = jnp.sum(match * cap_blocks[None, None, :], axis=2) * block_rows
    flat_match = match.reshape(row_count * top_count, replicas)
    before = jnp.cumsum(flat_match, axis=0) - flat_match
    arrival = jnp.sum(before * flat_match, axis=1).reshape(row_count, top_count)
    is_kept = arrival < capacity
    holder = replica_slot // slots
    within = replica_slot % slots
    position = within * (n_tensor * capacity_rows) + holder * capacity_rows + arrival
    position = jnp.where(is_kept, position, -1)
    buffer_rows = slots * n_tensor * capacity_rows
    placer = jnp.sum(
        (jnp.arange(buffer_rows, dtype=jnp.int32)[:, None, None] == position[None, :, :]).astype(
            jnp.bfloat16
        ),
        axis=2,
    )
    send_rows = jnp.dot(placer, normed, preferred_element_type=jnp.float32).astype(jnp.bfloat16)
    send_rows = send_rows.reshape(slots, n_tensor, capacity_rows, model_width)
    exchanged = lax.all_to_all(send_rows, TENSOR, split_axis=1, concat_axis=1, tiled=True)
    arrived = lax.all_gather(exchanged[None], "expert", axis=0, tiled=True)
    hidden = activate(arrived, w_gate_up)
    row_block = hidden
    summed = lax.psum_scatter(
        jnp.einsum("bsf,sfd->bsd", row_block, w_down, preferred_element_type=jnp.float32).astype(
            jnp.bfloat16
        ),
        "expert",
        scatter_dimension=0,
        tiled=True,
    )
    results = summed.reshape(n_tensor, capacity_rows, slots, model_width)
    returned = lax.all_to_all(results, TENSOR, split_axis=0, concat_axis=0, tiled=True)
    flat_back = returned.reshape(n_tensor * capacity_rows * slots, model_width)
    back_index = jnp.where(is_kept, holder * (capacity_rows * slots) + arrival * slots + within, 0)
    fetched = (
        jnp.take(flat_back, back_index.reshape(-1), axis=0)
        .reshape(row_count, top_count, model_width)
        .astype(jnp.float32)
    )
    factors = gate_mlp * is_kept.astype(jnp.float32)
    expert_mix = fetched[:, 0, :] * factors[:, 0:1] + fetched[:, 1, :] * factors[:, 1:2]
    after = stream.astype(jnp.float32) + expert_mix
    return (after.astype(jnp.bfloat16), rms_norm(after, final_gain).astype(jnp.bfloat16))


def split_mesh(mesh):
    n_expert, n_tensor = mesh.devices.shape
    n_y = 4 if n_tensor % 4 == 0 else 1
    return Mesh(mesh.devices.reshape(n_expert, n_tensor // n_y, n_y), ("expert", "tz", "ty"))


def solution(mesh):
    mesh = split_mesh(mesh)
    return jax.shard_map(
        per_device,
        mesh=mesh,
        in_specs=(
            P(("expert", "tz", "ty"), None),
            P("expert", TENSOR),
            P("expert", None),
            P("expert", None),
            P(None, TENSOR, None),
            P(),
            P(),
            P(("expert", "tz", "ty"), None),
            P(("expert", "tz", "ty"), None),
            P(),
            P(),
            P(TENSOR, None, None, "expert"),
            P(TENSOR, "expert", None),
            P(),
        ),
        out_specs=(P(("expert", "tz", "ty"), None), P(("expert", "tz", "ty"), None)),
        check_vma=False,
    )
```

```python
import jax
import jax.numpy as jnp
from jax import lax
from jax.sharding import Mesh, PartitionSpec as P

MAXB = 2
TENSOR = ("tz", "ty")


norm_eps = 1e-06


def rms_norm(values, gain):
    scale = lax.rsqrt(jnp.mean(values * values, axis=-1, keepdims=True) + norm_eps)
    return values * scale * gain.astype(values.dtype)


def pair_gates(scores):
    first = jax.nn.sigmoid(scores[:, 0] - scores[:, 1])
    return jnp.stack([first, 1.0 - first], axis=1)


def per_device(
    resid,
    contexts,
    att_routes,
    att_scores,
    att_out_w,
    norm_gain,
    router_w,
    mlp_routes,
    split_rule,
    placement,
    cap_blocks,
    w_gate_up,
    w_down,
    final_gain,
):
    n_tensor = lax.axis_size(TENSOR)
    row_count = resid.shape[0]
    model_width = resid.shape[1]
    group_rows = contexts.shape[0]
    att_experts = att_out_w.shape[0]
    slice_ctx = att_out_w.shape[1]
    top_count = att_routes.shape[1]
    gate_att = pair_gates(att_scores)
    width = att_experts * slice_ctx
    column = jnp.arange(width, dtype=jnp.int32)
    source = jnp.arange(slice_ctx * top_count, dtype=jnp.int32)[:, None]
    mixed = jnp.zeros((group_rows, width), jnp.float32)
    for choice in range(top_count):
        spread = (source == (column % slice_ctx)[None, :] * top_count + choice).astype(jnp.bfloat16)
        picked = jnp.dot(contexts, spread, preferred_element_type=jnp.float32)
        chosen = att_routes[:, choice : choice + 1] == (column // slice_ctx)[None, :]
        mixed = mixed + jnp.where(chosen, picked * gate_att[:, choice : choice + 1], 0.0)
    row_block = mixed.astype(jnp.bfloat16)
    weight_flat = att_out_w.reshape(width, model_width)
    partial = jnp.dot(row_block, weight_flat, preferred_element_type=jnp.float32).astype(jnp.bfloat16)
    partial = lax.psum_scatter(partial, "tz", scatter_dimension=0, tiled=True)
    attention = lax.psum_scatter(partial, "ty", scatter_dimension=0, tiled=True).astype(jnp.float32)
    stream = (resid.astype(jnp.float32) + attention).astype(jnp.bfloat16)
    normed = rms_norm(stream.astype(jnp.float32), norm_gain).astype(jnp.bfloat16)
    logits = jnp.dot(normed, router_w, preferred_element_type=jnp.float32)
    gate_mlp = pair_gates(jnp.take_along_axis(logits, mlp_routes, axis=1))
    replicas = placement.shape[0]
    slots = w_gate_up.shape[0]
    expert_total = router_w.shape[1]
    block_rows = max(1, row_count * top_count // (2 * replicas))
    capacity_rows = MAXB * block_rows
    slot_ids = jnp.arange(replicas, dtype=jnp.int32)
    expert_ids = jnp.arange(expert_total, dtype=jnp.int32)
    copies = jnp.sum((placement[None, :] == expert_ids[:, None]).astype(jnp.int32), axis=1)
    earlier = jnp.sum(
        (
            (placement[None, :] == placement[:, None]) & (slot_ids[None, :] < slot_ids[:, None])
        ).astype(jnp.int32),
        axis=1,
    )
    route_onehot = (mlp_routes[:, :, None] == expert_ids[None, None, :]).astype(jnp.int32)
    route_copies = jnp.sum(route_onehot * copies[None, None, :], axis=2)
    replica_rank = jnp.remainder(split_rule, route_copies)
    match = (
        (placement[None, None, :] == mlp_routes[:, :, None])
        & (earlier[None, None, :] == replica_rank[:, :, None])
    ).astype(jnp.int32)
    replica_slot = jnp.sum(match * slot_ids[None, None, :], axis=2)
    capacity = jnp.sum(match * cap_blocks[None, None, :], axis=2) * block_rows
    flat_match = match.reshape(row_count * top_count, replicas)
    before = jnp.cumsum(flat_match, axis=0) - flat_match
    arrival = jnp.sum(before * flat_match, axis=1).reshape(row_count, top_count)
    is_kept = arrival < capacity
    holder = replica_slot // slots
    within = replica_slot % slots
    position = within * (n_tensor * capacity_rows) + holder * capacity_rows + arrival
    position = jnp.where(is_kept, position, -1)
    buffer_rows = slots * n_tensor * capacity_rows
    placer = jnp.sum(
        (jnp.arange(buffer_rows, dtype=jnp.int32)[:, None, None] == position[None, :, :]).astype(
            jnp.bfloat16
        ),
        axis=2,
    )
    send_rows = jnp.dot(placer, normed, preferred_element_type=jnp.float32).astype(jnp.bfloat16)
    send_rows = send_rows.reshape(slots, n_tensor, capacity_rows, model_width)
    exchanged = lax.all_to_all(send_rows, TENSOR, split_axis=1, concat_axis=1, tiled=True)
    arrived = lax.all_gather(exchanged[None], "expert", axis=0, tiled=True)
    hidden_units = w_gate_up.shape[3]
    rows_in = arrived.reshape(-1, model_width)
    both = jnp.dot(
        rows_in, w_gate_up.reshape(model_width, 2 * hidden_units), preferred_element_type=jnp.float32
    )
    hidden = (jax.nn.silu(both[:, :hidden_units]) * both[:, hidden_units:]).astype(jnp.bfloat16)
    down = jnp.dot(
        hidden, w_down.reshape(hidden_units, model_width), preferred_element_type=jnp.float32
    ).astype(jnp.bfloat16)
    summed = lax.psum_scatter(down, "expert", scatter_dimension=0, tiled=True)
    results = summed.reshape(n_tensor, capacity_rows * slots, model_width)
    returned = lax.all_to_all(results, TENSOR, split_axis=0, concat_axis=0, tiled=True)
    flat_back = returned.reshape(n_tensor * capacity_rows * slots, model_width)
    back_index = jnp.where(is_kept, holder * (capacity_rows * slots) + arrival * slots + within, 0)
    factors = gate_mlp * is_kept.astype(jnp.float32)
    back_rows = flat_back.shape[0]
    select = jnp.sum(
        jnp.where(
            back_index[:, :, None] == jnp.arange(back_rows, dtype=jnp.int32)[None, None, :],
            factors[:, :, None],
            0.0,
        ),
        axis=1,
    )
    expert_mix = jnp.dot(
        select, flat_back.astype(jnp.float32), precision=lax.Precision.HIGHEST,
        preferred_element_type=jnp.float32,
    )
    after = stream.astype(jnp.float32) + expert_mix
    return (after.astype(jnp.bfloat16), rms_norm(after, final_gain).astype(jnp.bfloat16))


def split_mesh(mesh):
    n_expert, n_tensor = mesh.devices.shape
    n_y = 4 if n_tensor % 4 == 0 else 1
    return Mesh(mesh.devices.reshape(n_expert, n_tensor // n_y, n_y), ("expert", "tz", "ty"))


def solution(mesh):
    mesh = split_mesh(mesh)
    return jax.shard_map(
        per_device,
        mesh=mesh,
        in_specs=(
            P(("expert", "tz", "ty"), None),
            P("expert", TENSOR),
            P("expert", None),
            P("expert", None),
            P(None, TENSOR, None),
            P(),
            P(),
            P(("expert", "tz", "ty"), None),
            P(("expert", "tz", "ty"), None),
            P(),
            P(),
            P(TENSOR, None, None, "expert"),
            P(TENSOR, "expert", None),
            P(),
        ),
        out_specs=(P(("expert", "tz", "ty"), None), P(("expert", "tz", "ty"), None)),
        check_vma=False,
    )
```

```python
import jax
import jax.numpy as jnp
from jax import lax
from jax.sharding import Mesh, PartitionSpec as P

MAXB = 2
TENSOR = ("tz", "ty")


norm_eps = 1e-06


def rms_norm(values, gain):
    scale = lax.rsqrt(jnp.mean(values * values, axis=-1, keepdims=True) + norm_eps)
    return values * scale * gain.astype(values.dtype)


def pair_gates(scores):
    first = jax.nn.sigmoid(scores[:, 0] - scores[:, 1])
    return jnp.stack([first, 1.0 - first], axis=1)


def per_device(
    resid,
    contexts,
    att_routes,
    att_scores,
    att_out_w,
    norm_gain,
    router_w,
    mlp_routes,
    split_rule,
    placement,
    cap_blocks,
    w_gate_up,
    w_down,
    final_gain,
):
    n_tensor = lax.axis_size(TENSOR)
    row_count = resid.shape[0]
    model_width = resid.shape[1]
    group_rows = contexts.shape[0]
    att_experts = att_out_w.shape[0]
    slice_ctx = att_out_w.shape[1]
    top_count = att_routes.shape[1]
    gate_att = pair_gates(att_scores)
    width = att_experts * slice_ctx
    column = jnp.arange(width, dtype=jnp.int32)
    source = jnp.arange(slice_ctx * top_count, dtype=jnp.int32)[:, None]
    mixed = jnp.zeros((group_rows, width), jnp.float32)
    for choice in range(top_count):
        spread = (source == (column % slice_ctx)[None, :] * top_count + choice).astype(jnp.bfloat16)
        picked = jnp.dot(contexts, spread, preferred_element_type=jnp.float32)
        chosen = att_routes[:, choice : choice + 1] == (column // slice_ctx)[None, :]
        mixed = mixed + jnp.where(chosen, picked * gate_att[:, choice : choice + 1], 0.0)
    row_block = mixed.astype(jnp.bfloat16)
    weight_flat = att_out_w.reshape(width, model_width)
    partial = jnp.dot(row_block, weight_flat, preferred_element_type=jnp.float32).astype(jnp.bfloat16)
    partial = lax.psum_scatter(partial, "tz", scatter_dimension=0, tiled=True)
    attention = lax.psum_scatter(partial, "ty", scatter_dimension=0, tiled=True).astype(jnp.float32)
    stream = (resid.astype(jnp.float32) + attention).astype(jnp.bfloat16)
    normed = rms_norm(stream.astype(jnp.float32), norm_gain).astype(jnp.bfloat16)
    logits = jnp.dot(normed, router_w, preferred_element_type=jnp.float32)
    gate_mlp = pair_gates(jnp.take_along_axis(logits, mlp_routes, axis=1))
    replicas = placement.shape[0]
    slots = w_gate_up.shape[0]
    expert_total = router_w.shape[1]
    block_rows = max(1, row_count * top_count // (2 * replicas))
    capacity_rows = MAXB * block_rows
    slot_ids = jnp.arange(replicas, dtype=jnp.int32)
    expert_ids = jnp.arange(expert_total, dtype=jnp.int32)
    copies = jnp.sum((placement[None, :] == expert_ids[:, None]).astype(jnp.int32), axis=1)
    earlier = jnp.sum(
        (
            (placement[None, :] == placement[:, None]) & (slot_ids[None, :] < slot_ids[:, None])
        ).astype(jnp.int32),
        axis=1,
    )
    route_onehot = (mlp_routes[:, :, None] == expert_ids[None, None, :]).astype(jnp.int32)
    route_copies = jnp.sum(route_onehot * copies[None, None, :], axis=2)
    replica_rank = jnp.remainder(split_rule, route_copies)
    match = (
        (placement[None, None, :] == mlp_routes[:, :, None])
        & (earlier[None, None, :] == replica_rank[:, :, None])
    ).astype(jnp.int32)
    replica_slot = jnp.sum(match * slot_ids[None, None, :], axis=2)
    capacity = jnp.sum(match * cap_blocks[None, None, :], axis=2) * block_rows
    flat_match = match.reshape(row_count * top_count, replicas)
    before = jnp.cumsum(flat_match, axis=0) - flat_match
    arrival = jnp.sum(before * flat_match, axis=1).reshape(row_count, top_count)
    is_kept = arrival < capacity
    holder = replica_slot // slots
    within = replica_slot % slots
    position = within * (n_tensor * capacity_rows) + holder * capacity_rows + arrival
    position = jnp.where(is_kept, position, -1)
    buffer_rows = slots * n_tensor * capacity_rows
    placer = jnp.sum(
        (jnp.arange(buffer_rows, dtype=jnp.int32)[:, None, None] == position[None, :, :]).astype(
            jnp.bfloat16
        ),
        axis=2,
    )
    send_rows = jnp.dot(placer, normed, preferred_element_type=jnp.float32).astype(jnp.bfloat16)
    exchanged = lax.all_to_all(send_rows, TENSOR, split_axis=0, concat_axis=0, tiled=True)
    arrived = lax.all_gather(exchanged, "expert", axis=0, tiled=True)
    hidden_units = w_gate_up.shape[3]
    rows_in = arrived.reshape(-1, model_width)
    both = jnp.dot(
        rows_in, w_gate_up.reshape(model_width, 2 * hidden_units), preferred_element_type=jnp.float32
    )
    hidden = (jax.nn.silu(both[:, :hidden_units]) * both[:, hidden_units:]).astype(jnp.bfloat16)
    down = jnp.dot(
        hidden, w_down.reshape(hidden_units, model_width), preferred_element_type=jnp.float32
    ).astype(jnp.bfloat16)
    summed = lax.psum_scatter(down, "expert", scatter_dimension=0, tiled=True)
    flat_back = lax.all_to_all(summed, TENSOR, split_axis=0, concat_axis=0, tiled=True)
    back_index = jnp.where(is_kept, holder * (capacity_rows * slots) + arrival * slots + within, 0)
    factors = gate_mlp * is_kept.astype(jnp.float32)
    back_rows = flat_back.shape[0]
    select = jnp.sum(
        jnp.where(
            back_index[:, :, None] == jnp.arange(back_rows, dtype=jnp.int32)[None, None, :],
            factors[:, :, None],
            0.0,
        ),
        axis=1,
    )
    expert_mix = jnp.dot(
        select, flat_back.astype(jnp.float32), precision=lax.Precision.HIGHEST,
        preferred_element_type=jnp.float32,
    )
    after = stream.astype(jnp.float32) + expert_mix
    return (after.astype(jnp.bfloat16), rms_norm(after, final_gain).astype(jnp.bfloat16))


def split_mesh(mesh):
    n_expert, n_tensor = mesh.devices.shape
    n_y = 4 if n_tensor % 4 == 0 else 1
    return Mesh(mesh.devices.reshape(n_expert, n_tensor // n_y, n_y), ("expert", "tz", "ty"))


def solution(mesh):
    mesh = split_mesh(mesh)
    return jax.shard_map(
        per_device,
        mesh=mesh,
        in_specs=(
            P(("expert", "tz", "ty"), None),
            P("expert", TENSOR),
            P("expert", None),
            P("expert", None),
            P(None, TENSOR, None),
            P(),
            P(),
            P(("expert", "tz", "ty"), None),
            P(("expert", "tz", "ty"), None),
            P(),
            P(),
            P(TENSOR, None, None, "expert"),
            P(TENSOR, "expert", None),
            P(),
        ),
        out_specs=(P(("expert", "tz", "ty"), None), P(("expert", "tz", "ty"), None)),
        check_vma=False,
    )
```

```python
import jax
import jax.numpy as jnp
from jax import lax
from jax.sharding import Mesh, PartitionSpec as P

MAXB = 2
TENSOR = ("tz", "ty")


norm_eps = 1e-06


def rms_norm(values, gain):
    scale = lax.rsqrt(jnp.mean(values * values, axis=-1, keepdims=True) + norm_eps)
    return values * scale * gain.astype(values.dtype)


def pair_gates(scores):
    first = jax.nn.sigmoid(scores[:, 0] - scores[:, 1])
    return jnp.stack([first, 1.0 - first], axis=1)


def per_device(
    resid,
    contexts,
    att_routes,
    att_scores,
    att_out_w,
    norm_gain,
    router_w,
    mlp_routes,
    split_rule,
    placement,
    cap_blocks,
    w_gate_up,
    w_down,
    final_gain,
):
    n_tensor = lax.axis_size(TENSOR)
    row_count = resid.shape[0]
    model_width = resid.shape[1]
    group_rows = contexts.shape[0]
    att_experts = att_out_w.shape[0]
    slice_ctx = att_out_w.shape[1]
    top_count = att_routes.shape[1]
    gate_att = pair_gates(att_scores)
    width = att_experts * slice_ctx
    column = jnp.arange(width, dtype=jnp.int32)
    source = jnp.arange(slice_ctx * top_count, dtype=jnp.int32)[:, None]
    mixed = jnp.zeros((group_rows, width), jnp.float32)
    for choice in range(top_count):
        spread = (source == (column % slice_ctx)[None, :] * top_count + choice).astype(jnp.bfloat16)
        picked = jnp.dot(contexts, spread, preferred_element_type=jnp.float32)
        chosen = att_routes[:, choice : choice + 1] == (column // slice_ctx)[None, :]
        mixed = mixed + jnp.where(chosen, picked * gate_att[:, choice : choice + 1], 0.0)
    row_block = mixed.astype(jnp.bfloat16)
    weight_flat = att_out_w.reshape(width, model_width)
    partial = jnp.dot(row_block, weight_flat, preferred_element_type=jnp.float32).astype(jnp.bfloat16)
    partial = lax.psum_scatter(partial, "tz", scatter_dimension=0, tiled=True)
    n_y = lax.axis_size("ty")
    gathered = lax.all_to_all(partial, "ty", split_axis=0, concat_axis=0, tiled=True)
    attention = jnp.sum(gathered.reshape(n_y, -1, model_width).astype(jnp.float32), axis=0)
    stream = (resid.astype(jnp.float32) + attention).astype(jnp.bfloat16)
    normed = rms_norm(stream.astype(jnp.float32), norm_gain).astype(jnp.bfloat16)
    logits = jnp.dot(normed, router_w, preferred_element_type=jnp.float32)
    gate_mlp = pair_gates(jnp.take_along_axis(logits, mlp_routes, axis=1))
    replicas = placement.shape[0]
    slots = w_gate_up.shape[0]
    expert_total = router_w.shape[1]
    block_rows = max(1, row_count * top_count // (2 * replicas))
    capacity_rows = MAXB * block_rows
    slot_ids = jnp.arange(replicas, dtype=jnp.int32)
    expert_ids = jnp.arange(expert_total, dtype=jnp.int32)
    copies = jnp.sum((placement[None, :] == expert_ids[:, None]).astype(jnp.int32), axis=1)
    earlier = jnp.sum(
        (
            (placement[None, :] == placement[:, None]) & (slot_ids[None, :] < slot_ids[:, None])
        ).astype(jnp.int32),
        axis=1,
    )
    route_onehot = (mlp_routes[:, :, None] == expert_ids[None, None, :]).astype(jnp.int32)
    route_copies = jnp.sum(route_onehot * copies[None, None, :], axis=2)
    replica_rank = jnp.remainder(split_rule, route_copies)
    match = (
        (placement[None, None, :] == mlp_routes[:, :, None])
        & (earlier[None, None, :] == replica_rank[:, :, None])
    ).astype(jnp.int32)
    replica_slot = jnp.sum(match * slot_ids[None, None, :], axis=2)
    capacity = jnp.sum(match * cap_blocks[None, None, :], axis=2) * block_rows
    flat_match = match.reshape(row_count * top_count, replicas)
    before = jnp.cumsum(flat_match, axis=0) - flat_match
    arrival = jnp.sum(before * flat_match, axis=1).reshape(row_count, top_count)
    is_kept = arrival < capacity
    holder = replica_slot // slots
    within = replica_slot % slots
    position = within * (n_tensor * capacity_rows) + holder * capacity_rows + arrival
    position = jnp.where(is_kept, position, -1)
    buffer_rows = slots * n_tensor * capacity_rows
    placer = jnp.sum(
        (jnp.arange(buffer_rows, dtype=jnp.int32)[:, None, None] == position[None, :, :]).astype(
            jnp.bfloat16
        ),
        axis=2,
    )
    send_rows = jnp.dot(placer, normed, preferred_element_type=jnp.float32).astype(jnp.bfloat16)
    exchanged = lax.all_to_all(send_rows, TENSOR, split_axis=0, concat_axis=0, tiled=True)
    arrived = lax.all_gather(exchanged, "expert", axis=0, tiled=True)
    hidden_units = w_gate_up.shape[3]
    rows_in = arrived.reshape(-1, model_width)
    both = jnp.dot(
        rows_in, w_gate_up.reshape(model_width, 2 * hidden_units), preferred_element_type=jnp.float32
    )
    hidden = (jax.nn.silu(both[:, :hidden_units]) * both[:, hidden_units:]).astype(jnp.bfloat16)
    down = jnp.dot(
        hidden, w_down.reshape(hidden_units, model_width), preferred_element_type=jnp.float32
    ).astype(jnp.bfloat16)
    summed = lax.psum_scatter(down, "expert", scatter_dimension=0, tiled=True)
    flat_back = lax.all_to_all(summed, TENSOR, split_axis=0, concat_axis=0, tiled=True)
    back_index = jnp.where(is_kept, holder * (capacity_rows * slots) + arrival * slots + within, 0)
    factors = gate_mlp * is_kept.astype(jnp.float32)
    back_rows = flat_back.shape[0]
    select = jnp.sum(
        jnp.where(
            back_index[:, :, None] == jnp.arange(back_rows, dtype=jnp.int32)[None, None, :],
            factors[:, :, None],
            0.0,
        ),
        axis=1,
    )
    expert_mix = jnp.dot(
        select, flat_back.astype(jnp.float32), precision=lax.Precision.HIGHEST,
        preferred_element_type=jnp.float32,
    )
    after = stream.astype(jnp.float32) + expert_mix
    return (after.astype(jnp.bfloat16), rms_norm(after, final_gain).astype(jnp.bfloat16))


def split_mesh(mesh):
    n_expert, n_tensor = mesh.devices.shape
    n_y = 4 if n_tensor % 4 == 0 else 1
    return Mesh(mesh.devices.reshape(n_expert, n_tensor // n_y, n_y), ("expert", "tz", "ty"))


def solution(mesh):
    mesh = split_mesh(mesh)
    return jax.shard_map(
        per_device,
        mesh=mesh,
        in_specs=(
            P(("expert", "tz", "ty"), None),
            P("expert", TENSOR),
            P("expert", None),
            P("expert", None),
            P(None, TENSOR, None),
            P(),
            P(),
            P(("expert", "tz", "ty"), None),
            P(("expert", "tz", "ty"), None),
            P(),
            P(),
            P(TENSOR, None, None, "expert"),
            P(TENSOR, "expert", None),
            P(),
        ),
        out_specs=(P(("expert", "tz", "ty"), None), P(("expert", "tz", "ty"), None)),
        check_vma=False,
    )
```

```python
import jax
import jax.numpy as jnp
from jax import lax
from jax.sharding import Mesh, PartitionSpec as P

MAXB = 2
TENSOR = ("tz", "ty")
Z_SHARE = 4


norm_eps = 1e-06


def rms_norm(values, gain):
    scale = lax.rsqrt(jnp.mean(values * values, axis=-1, keepdims=True) + norm_eps)
    return values * scale * gain.astype(values.dtype)


def pair_gates(scores):
    first = jax.nn.sigmoid(scores[:, 0] - scores[:, 1])
    return jnp.stack([first, 1.0 - first], axis=1)


def per_device(
    resid,
    contexts,
    att_routes,
    att_scores,
    att_out_w,
    norm_gain,
    router_w,
    mlp_routes,
    split_rule,
    placement,
    cap_blocks,
    w_gate_up,
    w_down,
    final_gain,
):
    n_tensor = lax.axis_size(TENSOR)
    row_count = resid.shape[0]
    model_width = resid.shape[1]
    group_rows = contexts.shape[0]
    att_experts = att_out_w.shape[0]
    slice_ctx = att_out_w.shape[1]
    top_count = att_routes.shape[1]
    gate_att = pair_gates(att_scores)
    width = att_experts * slice_ctx
    column = jnp.arange(width, dtype=jnp.int32)
    source = jnp.arange(slice_ctx * top_count, dtype=jnp.int32)[:, None]
    mixed = jnp.zeros((group_rows, width), jnp.float32)
    for choice in range(top_count):
        spread = (source == (column % slice_ctx)[None, :] * top_count + choice).astype(jnp.bfloat16)
        picked = jnp.dot(contexts, spread, preferred_element_type=jnp.float32)
        chosen = att_routes[:, choice : choice + 1] == (column // slice_ctx)[None, :]
        mixed = mixed + jnp.where(chosen, picked * gate_att[:, choice : choice + 1], 0.0)
    row_block = mixed.astype(jnp.bfloat16)
    weight_flat = att_out_w.reshape(width, model_width)
    n_y = lax.axis_size("ty")
    n_z = lax.axis_size("tz")
    split = model_width * Z_SHARE // 8
    z_first = jnp.dot(row_block, weight_flat[:, :split], preferred_element_type=jnp.float32)
    z_first = lax.psum_scatter(z_first.astype(jnp.bfloat16), "tz", scatter_dimension=0, tiled=True)
    z_first = lax.all_to_all(z_first, "ty", split_axis=0, concat_axis=0, tiled=True)
    z_first = jnp.sum(z_first.reshape(n_y, -1, split).astype(jnp.float32), axis=0)
    by_y = row_block.reshape(n_z, n_y, -1, width).transpose(1, 0, 2, 3).reshape(group_rows, width)
    y_first = jnp.dot(by_y, weight_flat[:, split:], preferred_element_type=jnp.float32)
    y_first = lax.all_to_all(y_first.astype(jnp.bfloat16), "ty", split_axis=0, concat_axis=0, tiled=True)
    y_first = jnp.sum(y_first.reshape(n_y, -1, model_width - split).astype(jnp.float32), axis=0)
    y_first = lax.psum_scatter(y_first.astype(jnp.bfloat16), "tz", scatter_dimension=0, tiled=True)
    attention = jnp.concatenate([z_first, y_first.astype(jnp.float32)], axis=1)
    stream = (resid.astype(jnp.float32) + attention).astype(jnp.bfloat16)
    normed = rms_norm(stream.astype(jnp.float32), norm_gain).astype(jnp.bfloat16)
    logits = jnp.dot(normed, router_w, preferred_element_type=jnp.float32)
    gate_mlp = pair_gates(jnp.take_along_axis(logits, mlp_routes, axis=1))
    replicas = placement.shape[0]
    slots = w_gate_up.shape[0]
    expert_total = router_w.shape[1]
    block_rows = max(1, row_count * top_count // (2 * replicas))
    capacity_rows = MAXB * block_rows
    slot_ids = jnp.arange(replicas, dtype=jnp.int32)
    expert_ids = jnp.arange(expert_total, dtype=jnp.int32)
    copies = jnp.sum((placement[None, :] == expert_ids[:, None]).astype(jnp.int32), axis=1)
    earlier = jnp.sum(
        (
            (placement[None, :] == placement[:, None]) & (slot_ids[None, :] < slot_ids[:, None])
        ).astype(jnp.int32),
        axis=1,
    )
    route_onehot = (mlp_routes[:, :, None] == expert_ids[None, None, :]).astype(jnp.int32)
    route_copies = jnp.sum(route_onehot * copies[None, None, :], axis=2)
    replica_rank = jnp.remainder(split_rule, route_copies)
    match = (
        (placement[None, None, :] == mlp_routes[:, :, None])
        & (earlier[None, None, :] == replica_rank[:, :, None])
    ).astype(jnp.int32)
    replica_slot = jnp.sum(match * slot_ids[None, None, :], axis=2)
    capacity = jnp.sum(match * cap_blocks[None, None, :], axis=2) * block_rows
    flat_match = match.reshape(row_count * top_count, replicas)
    before = jnp.cumsum(flat_match, axis=0) - flat_match
    arrival = jnp.sum(before * flat_match, axis=1).reshape(row_count, top_count)
    is_kept = arrival < capacity
    holder = replica_slot // slots
    within = replica_slot % slots
    position = within * (n_tensor * capacity_rows) + holder * capacity_rows + arrival
    position = jnp.where(is_kept, position, -1)
    buffer_rows = slots * n_tensor * capacity_rows
    placer = jnp.sum(
        (jnp.arange(buffer_rows, dtype=jnp.int32)[:, None, None] == position[None, :, :]).astype(
            jnp.bfloat16
        ),
        axis=2,
    )
    send_rows = jnp.dot(placer, normed, preferred_element_type=jnp.float32).astype(jnp.bfloat16)
    exchanged = lax.all_to_all(send_rows, TENSOR, split_axis=0, concat_axis=0, tiled=True)
    arrived = lax.all_gather(exchanged, "expert", axis=0, tiled=True)
    hidden_units = w_gate_up.shape[3]
    rows_in = arrived.reshape(-1, model_width)
    both = jnp.dot(
        rows_in, w_gate_up.reshape(model_width, 2 * hidden_units), preferred_element_type=jnp.float32
    )
    hidden = (jax.nn.silu(both[:, :hidden_units]) * both[:, hidden_units:]).astype(jnp.bfloat16)
    down = jnp.dot(
        hidden, w_down.reshape(hidden_units, model_width), preferred_element_type=jnp.float32
    ).astype(jnp.bfloat16)
    summed = lax.psum_scatter(down, "expert", scatter_dimension=0, tiled=True)
    flat_back = lax.all_to_all(summed, TENSOR, split_axis=0, concat_axis=0, tiled=True)
    back_index = jnp.where(is_kept, holder * (capacity_rows * slots) + arrival * slots + within, 0)
    factors = gate_mlp * is_kept.astype(jnp.float32)
    back_rows = flat_back.shape[0]
    select = jnp.sum(
        jnp.where(
            back_index[:, :, None] == jnp.arange(back_rows, dtype=jnp.int32)[None, None, :],
            factors[:, :, None],
            0.0,
        ),
        axis=1,
    )
    expert_mix = jnp.dot(
        select, flat_back.astype(jnp.float32), precision=lax.Precision.HIGHEST,
        preferred_element_type=jnp.float32,
    )
    after = stream.astype(jnp.float32) + expert_mix
    return (after.astype(jnp.bfloat16), rms_norm(after, final_gain).astype(jnp.bfloat16))


def split_mesh(mesh):
    n_expert, n_tensor = mesh.devices.shape
    n_y = 4 if n_tensor % 4 == 0 else 1
    return Mesh(mesh.devices.reshape(n_expert, n_tensor // n_y, n_y), ("expert", "tz", "ty"))


def solution(mesh):
    mesh = split_mesh(mesh)
    return jax.shard_map(
        per_device,
        mesh=mesh,
        in_specs=(
            P(("expert", "tz", "ty"), None),
            P("expert", TENSOR),
            P("expert", None),
            P("expert", None),
            P(None, TENSOR, None),
            P(),
            P(),
            P(("expert", "tz", "ty"), None),
            P(("expert", "tz", "ty"), None),
            P(),
            P(),
            P(TENSOR, None, None, "expert"),
            P(TENSOR, "expert", None),
            P(),
        ),
        out_specs=(P(("expert", "tz", "ty"), None), P(("expert", "tz", "ty"), None)),
        check_vma=False,
    )
```

```python
import jax
import jax.numpy as jnp
from jax import lax
from jax.sharding import Mesh, PartitionSpec as P

MAXB = 2
TENSOR = ("tz", "ty")
EXPERT = ("ex", "ec")
ALL = ("ex", "ec", "tz", "ty")
Z_SHARE = 4


norm_eps = 1e-06


def rms_norm(values, gain):
    scale = lax.rsqrt(jnp.mean(values * values, axis=-1, keepdims=True) + norm_eps)
    return values * scale * gain.astype(values.dtype)


def pair_gates(scores):
    first = jax.nn.sigmoid(scores[:, 0] - scores[:, 1])
    return jnp.stack([first, 1.0 - first], axis=1)


def per_device(
    resid,
    contexts,
    att_routes,
    att_scores,
    att_out_w,
    norm_gain,
    router_w,
    mlp_routes,
    split_rule,
    placement,
    cap_blocks,
    w_gate_up,
    w_down,
    final_gain,
):
    n_tensor = lax.axis_size(TENSOR)
    row_count = resid.shape[0]
    model_width = resid.shape[1]
    group_rows = contexts.shape[0]
    att_experts = att_out_w.shape[0]
    slice_ctx = att_out_w.shape[1]
    top_count = att_routes.shape[1]
    gate_att = pair_gates(att_scores)
    width = att_experts * slice_ctx
    column = jnp.arange(width, dtype=jnp.int32)
    source = jnp.arange(slice_ctx * top_count, dtype=jnp.int32)[:, None]
    mixed = jnp.zeros((group_rows, width), jnp.float32)
    for choice in range(top_count):
        spread = (source == (column % slice_ctx)[None, :] * top_count + choice).astype(jnp.bfloat16)
        picked = jnp.dot(contexts, spread, preferred_element_type=jnp.float32)
        chosen = att_routes[:, choice : choice + 1] == (column // slice_ctx)[None, :]
        mixed = mixed + jnp.where(chosen, picked * gate_att[:, choice : choice + 1], 0.0)
    row_block = mixed.astype(jnp.bfloat16)
    weight_flat = att_out_w.reshape(width, model_width)
    n_y = lax.axis_size("ty")
    n_z = lax.axis_size("tz")
    split = model_width * Z_SHARE // 8
    z_first = jnp.dot(row_block, weight_flat[:, :split], preferred_element_type=jnp.float32)
    z_first = lax.psum_scatter(z_first.astype(jnp.bfloat16), "tz", scatter_dimension=0, tiled=True)
    z_first = lax.all_to_all(z_first, "ty", split_axis=0, concat_axis=0, tiled=True)
    z_first = jnp.sum(z_first.reshape(n_y, -1, split).astype(jnp.float32), axis=0)
    by_y = row_block.reshape(n_z, n_y, -1, width).transpose(1, 0, 2, 3).reshape(group_rows, width)
    y_first = jnp.dot(by_y, weight_flat[:, split:], preferred_element_type=jnp.float32)
    y_first = lax.all_to_all(y_first.astype(jnp.bfloat16), "ty", split_axis=0, concat_axis=0, tiled=True)
    y_first = jnp.sum(y_first.reshape(n_y, -1, model_width - split).astype(jnp.float32), axis=0)
    y_first = lax.psum_scatter(y_first.astype(jnp.bfloat16), "tz", scatter_dimension=0, tiled=True)
    attention = jnp.concatenate([z_first, y_first.astype(jnp.float32)], axis=1)
    stream = (resid.astype(jnp.float32) + attention).astype(jnp.bfloat16)
    normed = rms_norm(stream.astype(jnp.float32), norm_gain).astype(jnp.bfloat16)
    logits = jnp.dot(normed, router_w, preferred_element_type=jnp.float32)
    gate_mlp = pair_gates(jnp.take_along_axis(logits, mlp_routes, axis=1))
    replicas = placement.shape[0]
    slots = w_gate_up.shape[0]
    expert_total = router_w.shape[1]
    block_rows = max(1, row_count * top_count // (2 * replicas))
    capacity_rows = MAXB * block_rows
    slot_ids = jnp.arange(replicas, dtype=jnp.int32)
    expert_ids = jnp.arange(expert_total, dtype=jnp.int32)
    copies = jnp.sum((placement[None, :] == expert_ids[:, None]).astype(jnp.int32), axis=1)
    earlier = jnp.sum(
        (
            (placement[None, :] == placement[:, None]) & (slot_ids[None, :] < slot_ids[:, None])
        ).astype(jnp.int32),
        axis=1,
    )
    route_onehot = (mlp_routes[:, :, None] == expert_ids[None, None, :]).astype(jnp.int32)
    route_copies = jnp.sum(route_onehot * copies[None, None, :], axis=2)
    replica_rank = jnp.remainder(split_rule, route_copies)
    match = (
        (placement[None, None, :] == mlp_routes[:, :, None])
        & (earlier[None, None, :] == replica_rank[:, :, None])
    ).astype(jnp.int32)
    replica_slot = jnp.sum(match * slot_ids[None, None, :], axis=2)
    capacity = jnp.sum(match * cap_blocks[None, None, :], axis=2) * block_rows
    flat_match = match.reshape(row_count * top_count, replicas)
    before = jnp.cumsum(flat_match, axis=0) - flat_match
    arrival = jnp.sum(before * flat_match, axis=1).reshape(row_count, top_count)
    is_kept = arrival < capacity
    holder = replica_slot // slots
    within = replica_slot % slots
    position = within * (n_tensor * capacity_rows) + holder * capacity_rows + arrival
    position = jnp.where(is_kept, position, -1)
    buffer_rows = slots * n_tensor * capacity_rows
    placer = jnp.sum(
        (jnp.arange(buffer_rows, dtype=jnp.int32)[:, None, None] == position[None, :, :]).astype(
            jnp.bfloat16
        ),
        axis=2,
    )
    send_rows = jnp.dot(placer, normed, preferred_element_type=jnp.float32).astype(jnp.bfloat16)
    exchanged = lax.all_to_all(send_rows, TENSOR, split_axis=0, concat_axis=0, tiled=True)
    arrived = lax.all_gather(exchanged, "ex", axis=0, tiled=True)
    swap = [(0, 1), (1, 0)]
    paired_gate_up = lax.ppermute(w_gate_up, "ec", swap)
    paired_down = lax.ppermute(w_down, "ec", swap)
    hidden_units = w_gate_up.shape[3]

    def expert_part(gate_up, down_w):
        both = jnp.dot(
            arrived, gate_up.reshape(model_width, 2 * hidden_units), preferred_element_type=jnp.float32
        )
        hidden = (jax.nn.silu(both[:, :hidden_units]) * both[:, hidden_units:]).astype(jnp.bfloat16)
        return jnp.dot(
            hidden, down_w.reshape(hidden_units, model_width), preferred_element_type=jnp.float32
        )

    down = expert_part(w_gate_up, w_down) + expert_part(paired_gate_up, paired_down)
    summed = lax.psum_scatter(down.astype(jnp.bfloat16), "ex", scatter_dimension=0, tiled=True)
    flat_back = lax.all_to_all(summed, TENSOR, split_axis=0, concat_axis=0, tiled=True)
    back_index = jnp.where(is_kept, holder * (capacity_rows * slots) + arrival * slots + within, 0)
    factors = gate_mlp * is_kept.astype(jnp.float32)
    back_rows = flat_back.shape[0]
    select = jnp.sum(
        jnp.where(
            back_index[:, :, None] == jnp.arange(back_rows, dtype=jnp.int32)[None, None, :],
            factors[:, :, None],
            0.0,
        ),
        axis=1,
    )
    expert_mix = jnp.dot(
        select, flat_back.astype(jnp.float32), precision=lax.Precision.HIGHEST,
        preferred_element_type=jnp.float32,
    )
    after = stream.astype(jnp.float32) + expert_mix
    return (after.astype(jnp.bfloat16), rms_norm(after, final_gain).astype(jnp.bfloat16))


def split_mesh(mesh):
    n_expert, n_tensor = mesh.devices.shape
    n_y = 4 if n_tensor % 4 == 0 else 1
    shape = (n_expert // 2, 2, n_tensor // n_y, n_y)
    return Mesh(mesh.devices.reshape(shape), ALL)


def solution(mesh):
    mesh = split_mesh(mesh)
    return jax.shard_map(
        per_device,
        mesh=mesh,
        in_specs=(
            P(ALL, None),
            P(EXPERT, TENSOR),
            P(EXPERT, None),
            P(EXPERT, None),
            P(None, TENSOR, None),
            P(),
            P(),
            P(ALL, None),
            P(ALL, None),
            P(),
            P(),
            P(TENSOR, None, None, EXPERT),
            P(TENSOR, EXPERT, None),
            P(),
        ),
        out_specs=(P(ALL, None), P(ALL, None)),
        check_vma=False,
    )
```

```python
import jax
import jax.numpy as jnp
from jax import lax
from jax.sharding import Mesh, PartitionSpec as P

MAXB = 2
TENSOR = ("tz", "ty")
EXPERT = ("ex", "ec")
ALL = ("ex", "ec", "tz", "ty")
Z_SHARE = 4


norm_eps = 1e-06


def rms_norm(values, gain):
    scale = lax.rsqrt(jnp.mean(values * values, axis=-1, keepdims=True) + norm_eps)
    return values * scale * gain.astype(values.dtype)


def pair_gates(scores):
    first = jax.nn.sigmoid(scores[:, 0] - scores[:, 1])
    return jnp.stack([first, 1.0 - first], axis=1)


def per_device(
    resid,
    contexts,
    att_routes,
    att_scores,
    att_out_w,
    norm_gain,
    router_w,
    mlp_routes,
    split_rule,
    placement,
    cap_blocks,
    w_gate_up,
    w_down,
    final_gain,
):
    n_tensor = lax.axis_size(TENSOR)
    row_count = resid.shape[0]
    model_width = resid.shape[1]
    group_rows = contexts.shape[0]
    att_experts = att_out_w.shape[0]
    slice_ctx = att_out_w.shape[1]
    top_count = att_routes.shape[1]
    gate_att = pair_gates(att_scores)
    width = att_experts * slice_ctx
    column = jnp.arange(width, dtype=jnp.int32)
    source = jnp.arange(slice_ctx * top_count, dtype=jnp.int32)[:, None]
    mixed = jnp.zeros((group_rows, width), jnp.float32)
    for choice in range(top_count):
        spread = (source == (column % slice_ctx)[None, :] * top_count + choice).astype(jnp.bfloat16)
        picked = jnp.dot(contexts, spread, preferred_element_type=jnp.float32)
        chosen = att_routes[:, choice : choice + 1] == (column // slice_ctx)[None, :]
        mixed = mixed + jnp.where(chosen, picked * gate_att[:, choice : choice + 1], 0.0)
    row_block = mixed.astype(jnp.bfloat16)
    weight_flat = att_out_w.reshape(width, model_width)
    n_y = lax.axis_size("ty")
    n_z = lax.axis_size("tz")
    split = model_width * Z_SHARE // 8
    z_first = jnp.dot(row_block, weight_flat[:, :split], preferred_element_type=jnp.float32)
    z_first = lax.psum_scatter(z_first.astype(jnp.bfloat16), "tz", scatter_dimension=0, tiled=True)
    z_first = lax.all_to_all(z_first, "ty", split_axis=0, concat_axis=0, tiled=True)
    z_first = jnp.sum(z_first.reshape(n_y, -1, split).astype(jnp.float32), axis=0)
    by_y = row_block.reshape(n_z, n_y, -1, width).transpose(1, 0, 2, 3).reshape(group_rows, width)
    y_first = jnp.dot(by_y, weight_flat[:, split:], preferred_element_type=jnp.float32)
    y_first = lax.all_to_all(y_first.astype(jnp.bfloat16), "ty", split_axis=0, concat_axis=0, tiled=True)
    y_first = jnp.sum(y_first.reshape(n_y, -1, model_width - split).astype(jnp.float32), axis=0)
    y_first = lax.all_to_all(y_first.astype(jnp.bfloat16), "tz", split_axis=0, concat_axis=0, tiled=True)
    y_first = jnp.sum(y_first.reshape(n_z, -1, model_width - split).astype(jnp.float32), axis=0)
    attention = jnp.concatenate([z_first, y_first], axis=1)
    stream = (resid.astype(jnp.float32) + attention).astype(jnp.bfloat16)
    normed = rms_norm(stream.astype(jnp.float32), norm_gain).astype(jnp.bfloat16)
    logits = jnp.dot(normed, router_w, preferred_element_type=jnp.float32)
    gate_mlp = pair_gates(jnp.take_along_axis(logits, mlp_routes, axis=1))
    replicas = placement.shape[0]
    slots = w_gate_up.shape[0]
    expert_total = router_w.shape[1]
    block_rows = max(1, row_count * top_count // (2 * replicas))
    capacity_rows = MAXB * block_rows
    slot_ids = jnp.arange(replicas, dtype=jnp.int32)
    expert_ids = jnp.arange(expert_total, dtype=jnp.int32)
    copies = jnp.sum((placement[None, :] == expert_ids[:, None]).astype(jnp.int32), axis=1)
    earlier = jnp.sum(
        (
            (placement[None, :] == placement[:, None]) & (slot_ids[None, :] < slot_ids[:, None])
        ).astype(jnp.int32),
        axis=1,
    )
    route_onehot = (mlp_routes[:, :, None] == expert_ids[None, None, :]).astype(jnp.int32)
    route_copies = jnp.sum(route_onehot * copies[None, None, :], axis=2)
    replica_rank = jnp.remainder(split_rule, route_copies)
    match = (
        (placement[None, None, :] == mlp_routes[:, :, None])
        & (earlier[None, None, :] == replica_rank[:, :, None])
    ).astype(jnp.int32)
    replica_slot = jnp.sum(match * slot_ids[None, None, :], axis=2)
    capacity = jnp.sum(match * cap_blocks[None, None, :], axis=2) * block_rows
    flat_match = match.reshape(row_count * top_count, replicas)
    before = jnp.cumsum(flat_match, axis=0) - flat_match
    arrival = jnp.sum(before * flat_match, axis=1).reshape(row_count, top_count)
    is_kept = arrival < capacity
    holder = replica_slot // slots
    within = replica_slot % slots
    position = within * (n_tensor * capacity_rows) + holder * capacity_rows + arrival
    position = jnp.where(is_kept, position, -1)
    buffer_rows = slots * n_tensor * capacity_rows
    placer = jnp.sum(
        (jnp.arange(buffer_rows, dtype=jnp.int32)[:, None, None] == position[None, :, :]).astype(
            jnp.bfloat16
        ),
        axis=2,
    )
    send_rows = jnp.dot(placer, normed, preferred_element_type=jnp.float32).astype(jnp.bfloat16)
    exchanged = lax.all_to_all(send_rows, TENSOR, split_axis=0, concat_axis=0, tiled=True)
    arrived = lax.all_gather(exchanged, "ex", axis=0, tiled=True)
    swap = [(0, 1), (1, 0)]
    paired_gate_up = lax.ppermute(w_gate_up, "ec", swap)
    paired_down = lax.ppermute(w_down, "ec", swap)
    hidden_units = w_gate_up.shape[3]

    def activate(gate_up):
        both = jnp.dot(
            arrived, gate_up.reshape(model_width, 2 * hidden_units), preferred_element_type=jnp.float32
        )
        return (jax.nn.silu(both[:, :hidden_units]) * both[:, hidden_units:]).astype(jnp.bfloat16)

    hidden = jnp.concatenate([activate(w_gate_up), activate(paired_gate_up)], axis=1)
    down_w = jnp.concatenate(
        [w_down.reshape(hidden_units, model_width), paired_down.reshape(hidden_units, model_width)], axis=0
    )
    down = jnp.dot(hidden, down_w, preferred_element_type=jnp.float32)
    summed = lax.psum_scatter(down.astype(jnp.bfloat16), "ex", scatter_dimension=0, tiled=True)
    flat_back = lax.all_to_all(summed, TENSOR, split_axis=0, concat_axis=0, tiled=True)
    back_index = jnp.where(is_kept, holder * (capacity_rows * slots) + arrival * slots + within, 0)
    factors = gate_mlp * is_kept.astype(jnp.float32)
    back_rows = flat_back.shape[0]
    select = jnp.sum(
        jnp.where(
            back_index[:, :, None] == jnp.arange(back_rows, dtype=jnp.int32)[None, None, :],
            factors[:, :, None],
            0.0,
        ),
        axis=1,
    )
    expert_mix = jnp.dot(
        select, flat_back.astype(jnp.float32), precision=lax.Precision.HIGHEST,
        preferred_element_type=jnp.float32,
    )
    after = stream.astype(jnp.float32) + expert_mix
    return (after.astype(jnp.bfloat16), rms_norm(after, final_gain).astype(jnp.bfloat16))


def split_mesh(mesh):
    n_expert, n_tensor = mesh.devices.shape
    n_y = 4 if n_tensor % 4 == 0 else 1
    shape = (n_expert // 2, 2, n_tensor // n_y, n_y)
    return Mesh(mesh.devices.reshape(shape), ALL)


def solution(mesh):
    mesh = split_mesh(mesh)
    return jax.shard_map(
        per_device,
        mesh=mesh,
        in_specs=(
            P(ALL, None),
            P(EXPERT, TENSOR),
            P(EXPERT, None),
            P(EXPERT, None),
            P(None, TENSOR, None),
            P(),
            P(),
            P(ALL, None),
            P(ALL, None),
            P(),
            P(),
            P(TENSOR, None, None, EXPERT),
            P(TENSOR, EXPERT, None),
            P(),
        ),
        out_specs=(P(ALL, None), P(ALL, None)),
        check_vma=False,
    )
```

```python
import jax
import jax.numpy as jnp
from jax import lax
from jax.sharding import Mesh, PartitionSpec as P

MAXB = 2
TENSOR = ("tz", "ty")
EXPERT = ("ex", "ec")
ALL = ("ex", "ec", "tz", "ty")
Z_SHARE = 4


norm_eps = 1e-06


def rms_norm(values, gain):
    scale = lax.rsqrt(jnp.mean(values * values, axis=-1, keepdims=True) + norm_eps)
    return values * scale * gain.astype(values.dtype)


def pair_gates(scores):
    first = jax.nn.sigmoid(scores[:, 0] - scores[:, 1])
    return jnp.stack([first, 1.0 - first], axis=1)


def per_device(
    resid,
    contexts,
    att_routes,
    att_scores,
    att_out_w,
    norm_gain,
    router_w,
    mlp_routes,
    split_rule,
    placement,
    cap_blocks,
    w_gate_up,
    w_down,
    final_gain,
):
    n_tensor = lax.axis_size(TENSOR)
    row_count = resid.shape[0]
    model_width = resid.shape[1]
    group_rows = contexts.shape[0]
    att_experts = att_out_w.shape[0]
    slice_ctx = att_out_w.shape[1]
    top_count = att_routes.shape[1]
    gate_att = pair_gates(att_scores)
    width = att_experts * slice_ctx
    column = jnp.arange(width, dtype=jnp.int32)
    source = jnp.arange(slice_ctx * top_count, dtype=jnp.int32)[:, None]

    def mix(ctx, routes, gates):
        mixed = jnp.zeros((group_rows, width), jnp.float32)
        for choice in range(top_count):
            spread = (source == (column % slice_ctx)[None, :] * top_count + choice).astype(jnp.bfloat16)
            picked = jnp.dot(ctx, spread, preferred_element_type=jnp.float32)
            chosen = routes[:, choice : choice + 1] == (column // slice_ctx)[None, :]
            mixed = mixed + jnp.where(chosen, picked * gates[:, choice : choice + 1], 0.0)
        return mixed.astype(jnp.bfloat16)

    n_y = lax.axis_size("ty")
    n_z = lax.axis_size("tz")

    def y_major(values):
        return values.reshape(n_z, n_y, -1, values.shape[1]).transpose(1, 0, 2, 3).reshape(values.shape)

    row_block = mix(contexts, att_routes, gate_att)
    by_y = mix(y_major(contexts), y_major(att_routes), y_major(gate_att))
    weight_flat = att_out_w.reshape(width, model_width)
    split = model_width * Z_SHARE // 8
    z_first = jnp.dot(row_block, weight_flat[:, :split], preferred_element_type=jnp.float32)
    z_first = lax.psum_scatter(z_first.astype(jnp.bfloat16), "tz", scatter_dimension=0, tiled=True)
    z_first = lax.all_to_all(z_first, "ty", split_axis=0, concat_axis=0, tiled=True)
    z_first = jnp.sum(z_first.reshape(n_y, -1, split).astype(jnp.float32), axis=0)
    y_first = jnp.dot(by_y, weight_flat[:, split:], preferred_element_type=jnp.float32)
    y_first = lax.all_to_all(y_first.astype(jnp.bfloat16), "ty", split_axis=0, concat_axis=0, tiled=True)
    y_first = jnp.sum(y_first.reshape(n_y, -1, model_width - split).astype(jnp.float32), axis=0)
    y_first = lax.psum_scatter(y_first.astype(jnp.bfloat16), "tz", scatter_dimension=0, tiled=True)
    attention = jnp.concatenate([z_first, y_first.astype(jnp.float32)], axis=1)
    stream = (resid.astype(jnp.float32) + attention).astype(jnp.bfloat16)
    normed = rms_norm(stream.astype(jnp.float32), norm_gain).astype(jnp.bfloat16)
    logits = jnp.dot(normed, router_w, preferred_element_type=jnp.float32)
    gate_mlp = pair_gates(jnp.take_along_axis(logits, mlp_routes, axis=1))
    replicas = placement.shape[0]
    slots = w_gate_up.shape[0]
    expert_total = router_w.shape[1]
    block_rows = max(1, row_count * top_count // (2 * replicas))
    capacity_rows = MAXB * block_rows
    slot_ids = jnp.arange(replicas, dtype=jnp.int32)
    expert_ids = jnp.arange(expert_total, dtype=jnp.int32)
    copies = jnp.sum((placement[None, :] == expert_ids[:, None]).astype(jnp.int32), axis=1)
    earlier = jnp.sum(
        (
            (placement[None, :] == placement[:, None]) & (slot_ids[None, :] < slot_ids[:, None])
        ).astype(jnp.int32),
        axis=1,
    )
    route_onehot = (mlp_routes[:, :, None] == expert_ids[None, None, :]).astype(jnp.int32)
    route_copies = jnp.sum(route_onehot * copies[None, None, :], axis=2)
    replica_rank = jnp.remainder(split_rule, route_copies)
    match = (
        (placement[None, None, :] == mlp_routes[:, :, None])
        & (earlier[None, None, :] == replica_rank[:, :, None])
    ).astype(jnp.int32)
    replica_slot = jnp.sum(match * slot_ids[None, None, :], axis=2)
    capacity = jnp.sum(match * cap_blocks[None, None, :], axis=2) * block_rows
    flat_match = match.reshape(row_count * top_count, replicas)
    before = jnp.cumsum(flat_match, axis=0) - flat_match
    arrival = jnp.sum(before * flat_match, axis=1).reshape(row_count, top_count)
    is_kept = arrival < capacity
    holder = replica_slot // slots
    within = replica_slot % slots
    position = within * (n_tensor * capacity_rows) + holder * capacity_rows + arrival
    position = jnp.where(is_kept, position, -1)
    buffer_rows = slots * n_tensor * capacity_rows
    placer = jnp.sum(
        (jnp.arange(buffer_rows, dtype=jnp.int32)[:, None, None] == position[None, :, :]).astype(
            jnp.bfloat16
        ),
        axis=2,
    )
    send_rows = jnp.dot(placer, normed, preferred_element_type=jnp.float32).astype(jnp.bfloat16)
    exchanged = lax.all_to_all(send_rows, TENSOR, split_axis=0, concat_axis=0, tiled=True)
    arrived = lax.all_gather(exchanged, "ex", axis=0, tiled=True)
    swap = [(0, 1), (1, 0)]
    paired_gate_up = lax.ppermute(w_gate_up, "ec", swap)
    paired_down = lax.ppermute(w_down, "ec", swap)
    hidden_units = w_gate_up.shape[3]

    def expert_part(gate_up, down_w):
        both = jnp.dot(
            arrived, gate_up.reshape(model_width, 2 * hidden_units), preferred_element_type=jnp.float32
        )
        hidden = (jax.nn.silu(both[:, :hidden_units]) * both[:, hidden_units:]).astype(jnp.bfloat16)
        return jnp.dot(
            hidden, down_w.reshape(hidden_units, model_width), preferred_element_type=jnp.float32
        )

    down = expert_part(w_gate_up, w_down) + expert_part(paired_gate_up, paired_down)
    summed = lax.psum_scatter(down.astype(jnp.bfloat16), "ex", scatter_dimension=0, tiled=True)
    flat_back = lax.all_to_all(summed, TENSOR, split_axis=0, concat_axis=0, tiled=True)
    back_index = jnp.where(is_kept, holder * (capacity_rows * slots) + arrival * slots + within, 0)
    factors = gate_mlp * is_kept.astype(jnp.float32)
    back_rows = flat_back.shape[0]
    select = jnp.sum(
        jnp.where(
            back_index[:, :, None] == jnp.arange(back_rows, dtype=jnp.int32)[None, None, :],
            factors[:, :, None],
            0.0,
        ),
        axis=1,
    )
    expert_mix = jnp.dot(
        select, flat_back.astype(jnp.float32), precision=lax.Precision.HIGHEST,
        preferred_element_type=jnp.float32,
    )
    after = stream.astype(jnp.float32) + expert_mix
    return (after.astype(jnp.bfloat16), rms_norm(after, final_gain).astype(jnp.bfloat16))


def split_mesh(mesh):
    n_expert, n_tensor = mesh.devices.shape
    n_y = 4 if n_tensor % 4 == 0 else 1
    shape = (n_expert // 2, 2, n_tensor // n_y, n_y)
    return Mesh(mesh.devices.reshape(shape), ALL)


def solution(mesh):
    mesh = split_mesh(mesh)
    return jax.shard_map(
        per_device,
        mesh=mesh,
        in_specs=(
            P(ALL, None),
            P(EXPERT, TENSOR),
            P(EXPERT, None),
            P(EXPERT, None),
            P(None, TENSOR, None),
            P(),
            P(),
            P(ALL, None),
            P(ALL, None),
            P(),
            P(),
            P(TENSOR, None, None, EXPERT),
            P(TENSOR, EXPERT, None),
            P(),
        ),
        out_specs=(P(ALL, None), P(ALL, None)),
        check_vma=False,
    )
```

```python
import jax
import jax.numpy as jnp
from jax import lax
from jax.sharding import Mesh, PartitionSpec as P

MAXB = 2
TENSOR = ("tz", "ty")
EXPERT = ("ex", "ec")
ALL = ("ex", "ec", "tz", "ty")
Z_SHARE = 9


norm_eps = 1e-06


def rms_norm(values, gain):
    scale = lax.rsqrt(jnp.mean(values * values, axis=-1, keepdims=True) + norm_eps)
    return values * scale * gain.astype(values.dtype)


def pair_gates(scores):
    first = jax.nn.sigmoid(scores[:, 0] - scores[:, 1])
    return jnp.stack([first, 1.0 - first], axis=1)


def per_device(
    resid,
    contexts,
    att_routes,
    att_scores,
    att_out_w,
    norm_gain,
    router_w,
    mlp_routes,
    split_rule,
    placement,
    cap_blocks,
    w_gate_up,
    w_down,
    final_gain,
):
    n_tensor = lax.axis_size(TENSOR)
    row_count = resid.shape[0]
    model_width = resid.shape[1]
    group_rows = contexts.shape[0]
    att_experts = att_out_w.shape[0]
    slice_ctx = att_out_w.shape[1]
    top_count = att_routes.shape[1]
    gate_att = pair_gates(att_scores)
    width = att_experts * slice_ctx
    column = jnp.arange(width, dtype=jnp.int32)
    source = jnp.arange(slice_ctx * top_count, dtype=jnp.int32)[:, None]
    mixed = jnp.zeros((group_rows, width), jnp.float32)
    for choice in range(top_count):
        spread = (source == (column % slice_ctx)[None, :] * top_count + choice).astype(jnp.bfloat16)
        picked = jnp.dot(contexts, spread, preferred_element_type=jnp.float32)
        chosen = att_routes[:, choice : choice + 1] == (column // slice_ctx)[None, :]
        mixed = mixed + jnp.where(chosen, picked * gate_att[:, choice : choice + 1], 0.0)
    row_block = mixed.astype(jnp.bfloat16)
    weight_flat = att_out_w.reshape(width, model_width)
    n_y = lax.axis_size("ty")
    n_z = lax.axis_size("tz")
    split = model_width * Z_SHARE // 16
    z_first = jnp.dot(row_block, weight_flat[:, :split], preferred_element_type=jnp.float32)
    z_first = lax.psum_scatter(z_first.astype(jnp.bfloat16), "tz", scatter_dimension=0, tiled=True)
    z_first = lax.all_to_all(z_first, "ty", split_axis=0, concat_axis=0, tiled=True)
    z_first = jnp.sum(z_first.reshape(n_y, -1, split).astype(jnp.float32), axis=0)
    by_y = row_block.reshape(n_z, n_y, -1, width).transpose(1, 0, 2, 3).reshape(group_rows, width)
    y_first = jnp.dot(by_y, weight_flat[:, split:], preferred_element_type=jnp.float32)
    y_first = lax.all_to_all(y_first.astype(jnp.bfloat16), "ty", split_axis=0, concat_axis=0, tiled=True)
    y_first = jnp.sum(y_first.reshape(n_y, -1, model_width - split).astype(jnp.float32), axis=0)
    y_first = lax.psum_scatter(y_first.astype(jnp.bfloat16), "tz", scatter_dimension=0, tiled=True)
    attention = jnp.concatenate([z_first, y_first.astype(jnp.float32)], axis=1)
    stream = (resid.astype(jnp.float32) + attention).astype(jnp.bfloat16)
    normed = rms_norm(stream.astype(jnp.float32), norm_gain).astype(jnp.bfloat16)
    logits = jnp.dot(normed, router_w, preferred_element_type=jnp.float32)
    gate_mlp = pair_gates(jnp.take_along_axis(logits, mlp_routes, axis=1))
    replicas = placement.shape[0]
    slots = w_gate_up.shape[0]
    expert_total = router_w.shape[1]
    block_rows = max(1, row_count * top_count // (2 * replicas))
    capacity_rows = MAXB * block_rows
    slot_ids = jnp.arange(replicas, dtype=jnp.int32)
    expert_ids = jnp.arange(expert_total, dtype=jnp.int32)
    copies = jnp.sum((placement[None, :] == expert_ids[:, None]).astype(jnp.int32), axis=1)
    earlier = jnp.sum(
        (
            (placement[None, :] == placement[:, None]) & (slot_ids[None, :] < slot_ids[:, None])
        ).astype(jnp.int32),
        axis=1,
    )
    route_onehot = (mlp_routes[:, :, None] == expert_ids[None, None, :]).astype(jnp.int32)
    route_copies = jnp.sum(route_onehot * copies[None, None, :], axis=2)
    replica_rank = jnp.remainder(split_rule, route_copies)
    match = (
        (placement[None, None, :] == mlp_routes[:, :, None])
        & (earlier[None, None, :] == replica_rank[:, :, None])
    ).astype(jnp.int32)
    replica_slot = jnp.sum(match * slot_ids[None, None, :], axis=2)
    capacity = jnp.sum(match * cap_blocks[None, None, :], axis=2) * block_rows
    flat_match = match.reshape(row_count * top_count, replicas)
    before = jnp.cumsum(flat_match, axis=0) - flat_match
    arrival = jnp.sum(before * flat_match, axis=1).reshape(row_count, top_count)
    is_kept = arrival < capacity
    holder = replica_slot // slots
    within = replica_slot % slots
    position = within * (n_tensor * capacity_rows) + holder * capacity_rows + arrival
    position = jnp.where(is_kept, position, -1)
    buffer_rows = slots * n_tensor * capacity_rows
    placer = jnp.sum(
        (jnp.arange(buffer_rows, dtype=jnp.int32)[:, None, None] == position[None, :, :]).astype(
            jnp.bfloat16
        ),
        axis=2,
    )
    send_rows = jnp.dot(placer, normed, preferred_element_type=jnp.float32).astype(jnp.bfloat16)
    exchanged = lax.all_to_all(send_rows, TENSOR, split_axis=0, concat_axis=0, tiled=True)
    arrived = lax.all_gather(exchanged, "ex", axis=0, tiled=True)
    swap = [(0, 1), (1, 0)]
    paired_gate_up = lax.ppermute(w_gate_up, "ec", swap)
    paired_down = lax.ppermute(w_down, "ec", swap)
    hidden_units = w_gate_up.shape[3]

    def expert_part(gate_up, down_w):
        both = jnp.dot(
            arrived, gate_up.reshape(model_width, 2 * hidden_units), preferred_element_type=jnp.float32
        )
        hidden = (jax.nn.silu(both[:, :hidden_units]) * both[:, hidden_units:]).astype(jnp.bfloat16)
        return jnp.dot(
            hidden, down_w.reshape(hidden_units, model_width), preferred_element_type=jnp.float32
        )

    down = expert_part(w_gate_up, w_down) + expert_part(paired_gate_up, paired_down)
    summed = lax.psum_scatter(down.astype(jnp.bfloat16), "ex", scatter_dimension=0, tiled=True)
    flat_back = lax.all_to_all(summed, TENSOR, split_axis=0, concat_axis=0, tiled=True)
    back_index = jnp.where(is_kept, holder * (capacity_rows * slots) + arrival * slots + within, 0)
    factors = gate_mlp * is_kept.astype(jnp.float32)
    back_rows = flat_back.shape[0]
    select = jnp.sum(
        jnp.where(
            back_index[:, :, None] == jnp.arange(back_rows, dtype=jnp.int32)[None, None, :],
            factors[:, :, None],
            0.0,
        ),
        axis=1,
    )
    expert_mix = jnp.dot(
        select, flat_back.astype(jnp.float32), precision=lax.Precision.HIGHEST,
        preferred_element_type=jnp.float32,
    )
    after = stream.astype(jnp.float32) + expert_mix
    return (after.astype(jnp.bfloat16), rms_norm(after, final_gain).astype(jnp.bfloat16))


def split_mesh(mesh):
    n_expert, n_tensor = mesh.devices.shape
    n_y = 4 if n_tensor % 4 == 0 else 1
    shape = (n_expert // 2, 2, n_tensor // n_y, n_y)
    return Mesh(mesh.devices.reshape(shape), ALL)


def solution(mesh):
    mesh = split_mesh(mesh)
    return jax.shard_map(
        per_device,
        mesh=mesh,
        in_specs=(
            P(ALL, None),
            P(EXPERT, TENSOR),
            P(EXPERT, None),
            P(EXPERT, None),
            P(None, TENSOR, None),
            P(),
            P(),
            P(ALL, None),
            P(ALL, None),
            P(),
            P(),
            P(TENSOR, None, None, EXPERT),
            P(TENSOR, EXPERT, None),
            P(),
        ),
        out_specs=(P(ALL, None), P(ALL, None)),
        check_vma=False,
    )
```

```python
import jax
import ml_dtypes
import numpy as np
import jax.numpy as jnp
from jax import lax
from jax.sharding import Mesh, PartitionSpec as P

MAXB = 2
TENSOR = ("tz", "ty")
EXPERT = ("ex", "ec")
ALL = ("ex", "ec", "tz", "ty")
Z_SHARE = 9


norm_eps = 1e-06


def rms_norm(values, gain):
    scale = lax.rsqrt(jnp.mean(values * values, axis=-1, keepdims=True) + norm_eps)
    return values * scale * gain.astype(values.dtype)


def pair_gates(scores):
    first = jax.nn.sigmoid(scores[:, 0] - scores[:, 1])
    return jnp.stack([first, 1.0 - first], axis=1)


def per_device(
    resid,
    contexts,
    att_routes,
    att_scores,
    att_out_w,
    norm_gain,
    router_w,
    mlp_routes,
    split_rule,
    placement,
    cap_blocks,
    w_gate_up,
    w_down,
    final_gain,
):
    n_tensor = lax.axis_size(TENSOR)
    row_count = resid.shape[0]
    model_width = resid.shape[1]
    group_rows = contexts.shape[0]
    att_experts = att_out_w.shape[0]
    slice_ctx = att_out_w.shape[1]
    top_count = att_routes.shape[1]
    gate_att = pair_gates(att_scores)
    width = att_experts * slice_ctx
    column = np.arange(width)
    source = np.arange(slice_ctx * top_count)[:, None]
    owner = jnp.asarray((column // slice_ctx)[None, :].astype(np.int32))
    mixed = jnp.zeros((group_rows, width), jnp.float32)
    for choice in range(top_count):
        spread = source == (column % slice_ctx)[None, :] * top_count + choice
        spread = jnp.asarray(spread.astype(ml_dtypes.bfloat16))
        picked = jnp.dot(contexts, spread, preferred_element_type=jnp.float32)
        chosen = att_routes[:, choice : choice + 1] == owner
        mixed = mixed + jnp.where(chosen, picked * gate_att[:, choice : choice + 1], 0.0)
    row_block = mixed.astype(jnp.bfloat16)
    weight_flat = att_out_w.reshape(width, model_width)
    n_y = lax.axis_size("ty")
    n_z = lax.axis_size("tz")
    split = model_width * Z_SHARE // 16
    z_first = jnp.dot(row_block, weight_flat[:, :split], preferred_element_type=jnp.float32)
    z_first = lax.psum_scatter(z_first.astype(jnp.bfloat16), "tz", scatter_dimension=0, tiled=True)
    z_first = lax.all_to_all(z_first, "ty", split_axis=0, concat_axis=0, tiled=True)
    z_first = jnp.sum(z_first.reshape(n_y, -1, split).astype(jnp.float32), axis=0)
    by_y = row_block.reshape(n_z, n_y, -1, width).transpose(1, 0, 2, 3).reshape(group_rows, width)
    y_first = jnp.dot(by_y, weight_flat[:, split:], preferred_element_type=jnp.float32)
    y_first = lax.all_to_all(y_first.astype(jnp.bfloat16), "ty", split_axis=0, concat_axis=0, tiled=True)
    y_first = jnp.sum(y_first.reshape(n_y, -1, model_width - split).astype(jnp.float32), axis=0)
    y_first = lax.psum_scatter(y_first.astype(jnp.bfloat16), "tz", scatter_dimension=0, tiled=True)
    attention = jnp.concatenate([z_first, y_first.astype(jnp.float32)], axis=1)
    stream = (resid.astype(jnp.float32) + attention).astype(jnp.bfloat16)
    normed = rms_norm(stream.astype(jnp.float32), norm_gain).astype(jnp.bfloat16)
    logits = jnp.dot(normed, router_w, preferred_element_type=jnp.float32)
    gate_mlp = pair_gates(jnp.take_along_axis(logits, mlp_routes, axis=1))
    replicas = placement.shape[0]
    slots = w_gate_up.shape[0]
    expert_total = router_w.shape[1]
    block_rows = max(1, row_count * top_count // (2 * replicas))
    capacity_rows = MAXB * block_rows
    slot_ids = jnp.arange(replicas, dtype=jnp.int32)
    expert_ids = jnp.arange(expert_total, dtype=jnp.int32)
    copies = jnp.sum((placement[None, :] == expert_ids[:, None]).astype(jnp.int32), axis=1)
    earlier = jnp.sum(
        (
            (placement[None, :] == placement[:, None]) & (slot_ids[None, :] < slot_ids[:, None])
        ).astype(jnp.int32),
        axis=1,
    )
    route_onehot = (mlp_routes[:, :, None] == expert_ids[None, None, :]).astype(jnp.int32)
    route_copies = jnp.sum(route_onehot * copies[None, None, :], axis=2)
    replica_rank = jnp.remainder(split_rule, route_copies)
    match = (
        (placement[None, None, :] == mlp_routes[:, :, None])
        & (earlier[None, None, :] == replica_rank[:, :, None])
    ).astype(jnp.int32)
    replica_slot = jnp.sum(match * slot_ids[None, None, :], axis=2)
    capacity = jnp.sum(match * cap_blocks[None, None, :], axis=2) * block_rows
    flat_match = match.reshape(row_count * top_count, replicas)
    before = jnp.cumsum(flat_match, axis=0) - flat_match
    arrival = jnp.sum(before * flat_match, axis=1).reshape(row_count, top_count)
    is_kept = arrival < capacity
    holder = replica_slot // slots
    within = replica_slot % slots
    position = within * (n_tensor * capacity_rows) + holder * capacity_rows + arrival
    position = jnp.where(is_kept, position, -1)
    buffer_rows = slots * n_tensor * capacity_rows
    placer = jnp.sum(
        (jnp.arange(buffer_rows, dtype=jnp.int32)[:, None, None] == position[None, :, :]).astype(
            jnp.bfloat16
        ),
        axis=2,
    )
    send_rows = jnp.dot(placer, normed, preferred_element_type=jnp.float32).astype(jnp.bfloat16)
    exchanged = lax.all_to_all(send_rows, TENSOR, split_axis=0, concat_axis=0, tiled=True)
    arrived = lax.all_gather(exchanged, "ex", axis=0, tiled=True)
    swap = [(0, 1), (1, 0)]
    paired_gate_up = lax.ppermute(w_gate_up, "ec", swap)
    paired_down = lax.ppermute(w_down, "ec", swap)
    hidden_units = w_gate_up.shape[3]

    def expert_part(gate_up, down_w):
        both = jnp.dot(
            arrived, gate_up.reshape(model_width, 2 * hidden_units), preferred_element_type=jnp.float32
        )
        hidden = (jax.nn.silu(both[:, :hidden_units]) * both[:, hidden_units:]).astype(jnp.bfloat16)
        return jnp.dot(
            hidden, down_w.reshape(hidden_units, model_width), preferred_element_type=jnp.float32
        )

    down = expert_part(w_gate_up, w_down) + expert_part(paired_gate_up, paired_down)
    summed = lax.psum_scatter(down.astype(jnp.bfloat16), "ex", scatter_dimension=0, tiled=True)
    flat_back = lax.all_to_all(summed, TENSOR, split_axis=0, concat_axis=0, tiled=True)
    back_index = jnp.where(is_kept, holder * (capacity_rows * slots) + arrival * slots + within, 0)
    factors = gate_mlp * is_kept.astype(jnp.float32)
    back_rows = flat_back.shape[0]
    select = jnp.sum(
        jnp.where(
            back_index[:, :, None] == jnp.arange(back_rows, dtype=jnp.int32)[None, None, :],
            factors[:, :, None],
            0.0,
        ),
        axis=1,
    )
    expert_mix = jnp.dot(
        select, flat_back.astype(jnp.float32), precision=lax.Precision.HIGHEST,
        preferred_element_type=jnp.float32,
    )
    after = stream.astype(jnp.float32) + expert_mix
    return (after.astype(jnp.bfloat16), rms_norm(after, final_gain).astype(jnp.bfloat16))


def split_mesh(mesh):
    n_expert, n_tensor = mesh.devices.shape
    n_y = 4 if n_tensor % 4 == 0 else 1
    shape = (n_expert // 2, 2, n_tensor // n_y, n_y)
    return Mesh(mesh.devices.reshape(shape), ALL)


def solution(mesh):
    mesh = split_mesh(mesh)
    return jax.shard_map(
        per_device,
        mesh=mesh,
        in_specs=(
            P(ALL, None),
            P(EXPERT, TENSOR),
            P(EXPERT, None),
            P(EXPERT, None),
            P(None, TENSOR, None),
            P(),
            P(),
            P(ALL, None),
            P(ALL, None),
            P(),
            P(),
            P(TENSOR, None, None, EXPERT),
            P(TENSOR, EXPERT, None),
            P(),
        ),
        out_specs=(P(ALL, None), P(ALL, None)),
        check_vma=False,
    )
```

```python
import jax
import jax.numpy as jnp
from jax import lax
from jax.sharding import Mesh, PartitionSpec as P

MAXB = 2
TENSOR = ("tz", "ty")
EXPERT = ("ex", "ec")
ALL = ("ex", "ec", "tz", "ty")
Z_SHARE = 9


norm_eps = 1e-06


def rms_norm(values, gain):
    scale = lax.rsqrt(jnp.mean(values * values, axis=-1, keepdims=True) + norm_eps)
    return values * scale * gain.astype(values.dtype)


def pair_gates(scores):
    first = jax.nn.sigmoid(scores[:, 0] - scores[:, 1])
    return jnp.stack([first, 1.0 - first], axis=1)


def per_device(
    resid,
    contexts,
    att_routes,
    att_scores,
    att_out_w,
    norm_gain,
    router_w,
    mlp_routes,
    split_rule,
    placement,
    cap_blocks,
    w_gate_up,
    w_down,
    final_gain,
):
    n_tensor = lax.axis_size(TENSOR)
    row_count = resid.shape[0]
    model_width = resid.shape[1]
    group_rows = contexts.shape[0]
    att_experts = att_out_w.shape[0]
    slice_ctx = att_out_w.shape[1]
    top_count = att_routes.shape[1]
    gate_att = pair_gates(att_scores)
    width = att_experts * slice_ctx
    column = jnp.arange(width, dtype=jnp.int32)
    source = jnp.arange(slice_ctx * top_count, dtype=jnp.int32)[:, None]
    mixed = jnp.zeros((group_rows, width), jnp.float32)
    for choice in range(top_count):
        spread = (source == (column % slice_ctx)[None, :] * top_count + choice).astype(jnp.bfloat16)
        picked = jnp.dot(contexts, spread, preferred_element_type=jnp.float32)
        chosen = att_routes[:, choice : choice + 1] == (column // slice_ctx)[None, :]
        mixed = mixed + jnp.where(chosen, picked * gate_att[:, choice : choice + 1], 0.0)
    row_block = mixed.astype(jnp.bfloat16)
    weight_flat = att_out_w.reshape(width, model_width)
    n_y = lax.axis_size("ty")
    n_z = lax.axis_size("tz")
    split = model_width * Z_SHARE // 16
    z_first = jnp.dot(row_block, weight_flat[:, :split], preferred_element_type=jnp.float32)
    z_first = lax.psum_scatter(z_first.astype(jnp.bfloat16), "tz", scatter_dimension=0, tiled=True)
    z_first = lax.psum_scatter(z_first, "ty", scatter_dimension=0, tiled=True).astype(jnp.float32)
    by_y = row_block.reshape(n_z, n_y, -1, width).transpose(1, 0, 2, 3).reshape(group_rows, width)
    y_first = jnp.dot(by_y, weight_flat[:, split:], preferred_element_type=jnp.float32)
    y_first = lax.all_to_all(y_first.astype(jnp.bfloat16), "ty", split_axis=0, concat_axis=0, tiled=True)
    y_first = jnp.sum(y_first.reshape(n_y, -1, model_width - split).astype(jnp.float32), axis=0)
    y_first = lax.all_to_all(y_first.astype(jnp.bfloat16), "tz", split_axis=0, concat_axis=0, tiled=True)
    y_first = jnp.sum(y_first.reshape(n_z, -1, model_width - split).astype(jnp.float32), axis=0)
    attention = jnp.concatenate([z_first, y_first], axis=1)
    stream = (resid.astype(jnp.float32) + attention).astype(jnp.bfloat16)
    normed = rms_norm(stream.astype(jnp.float32), norm_gain).astype(jnp.bfloat16)
    logits = jnp.dot(normed, router_w, preferred_element_type=jnp.float32)
    gate_mlp = pair_gates(jnp.take_along_axis(logits, mlp_routes, axis=1))
    replicas = placement.shape[0]
    slots = w_gate_up.shape[0]
    expert_total = router_w.shape[1]
    block_rows = max(1, row_count * top_count // (2 * replicas))
    capacity_rows = MAXB * block_rows
    slot_ids = jnp.arange(replicas, dtype=jnp.int32)
    expert_ids = jnp.arange(expert_total, dtype=jnp.int32)
    copies = jnp.sum((placement[None, :] == expert_ids[:, None]).astype(jnp.int32), axis=1)
    earlier = jnp.sum(
        (
            (placement[None, :] == placement[:, None]) & (slot_ids[None, :] < slot_ids[:, None])
        ).astype(jnp.int32),
        axis=1,
    )
    route_onehot = (mlp_routes[:, :, None] == expert_ids[None, None, :]).astype(jnp.int32)
    route_copies = jnp.sum(route_onehot * copies[None, None, :], axis=2)
    replica_rank = jnp.remainder(split_rule, route_copies)
    match = (
        (placement[None, None, :] == mlp_routes[:, :, None])
        & (earlier[None, None, :] == replica_rank[:, :, None])
    ).astype(jnp.int32)
    replica_slot = jnp.sum(match * slot_ids[None, None, :], axis=2)
    capacity = jnp.sum(match * cap_blocks[None, None, :], axis=2) * block_rows
    flat_match = match.reshape(row_count * top_count, replicas)
    before = jnp.cumsum(flat_match, axis=0) - flat_match
    arrival = jnp.sum(before * flat_match, axis=1).reshape(row_count, top_count)
    is_kept = arrival < capacity
    holder = replica_slot // slots
    within = replica_slot % slots
    position = within * (n_tensor * capacity_rows) + holder * capacity_rows + arrival
    position = jnp.where(is_kept, position, -1)
    buffer_rows = slots * n_tensor * capacity_rows
    placer = jnp.sum(
        (jnp.arange(buffer_rows, dtype=jnp.int32)[:, None, None] == position[None, :, :]).astype(
            jnp.bfloat16
        ),
        axis=2,
    )
    send_rows = jnp.dot(placer, normed, preferred_element_type=jnp.float32).astype(jnp.bfloat16)
    exchanged = lax.all_to_all(send_rows, TENSOR, split_axis=0, concat_axis=0, tiled=True)
    arrived = lax.all_gather(exchanged, "ex", axis=0, tiled=True)
    swap = [(0, 1), (1, 0)]
    paired_gate_up = lax.ppermute(w_gate_up, "ec", swap)
    paired_down = lax.ppermute(w_down, "ec", swap)
    hidden_units = w_gate_up.shape[3]

    def expert_part(gate_up, down_w):
        both = jnp.dot(
            arrived, gate_up.reshape(model_width, 2 * hidden_units), preferred_element_type=jnp.float32
        )
        hidden = (jax.nn.silu(both[:, :hidden_units]) * both[:, hidden_units:]).astype(jnp.bfloat16)
        return jnp.dot(
            hidden, down_w.reshape(hidden_units, model_width), preferred_element_type=jnp.float32
        )

    down = expert_part(w_gate_up, w_down) + expert_part(paired_gate_up, paired_down)
    summed = lax.psum_scatter(down.astype(jnp.bfloat16), "ex", scatter_dimension=0, tiled=True)
    flat_back = lax.all_to_all(summed, TENSOR, split_axis=0, concat_axis=0, tiled=True)
    back_index = jnp.where(is_kept, holder * (capacity_rows * slots) + arrival * slots + within, 0)
    factors = gate_mlp * is_kept.astype(jnp.float32)
    back_rows = flat_back.shape[0]
    select = jnp.sum(
        jnp.where(
            back_index[:, :, None] == jnp.arange(back_rows, dtype=jnp.int32)[None, None, :],
            factors[:, :, None],
            0.0,
        ),
        axis=1,
    )
    expert_mix = jnp.dot(
        select, flat_back.astype(jnp.float32), precision=lax.Precision.HIGHEST,
        preferred_element_type=jnp.float32,
    )
    after = stream.astype(jnp.float32) + expert_mix
    return (after.astype(jnp.bfloat16), rms_norm(after, final_gain).astype(jnp.bfloat16))


def split_mesh(mesh):
    n_expert, n_tensor = mesh.devices.shape
    n_y = 4 if n_tensor % 4 == 0 else 1
    shape = (n_expert // 2, 2, n_tensor // n_y, n_y)
    return Mesh(mesh.devices.reshape(shape), ALL)


def solution(mesh):
    mesh = split_mesh(mesh)
    return jax.shard_map(
        per_device,
        mesh=mesh,
        in_specs=(
            P(ALL, None),
            P(EXPERT, TENSOR),
            P(EXPERT, None),
            P(EXPERT, None),
            P(None, TENSOR, None),
            P(),
            P(),
            P(ALL, None),
            P(ALL, None),
            P(),
            P(),
            P(TENSOR, None, None, EXPERT),
            P(TENSOR, EXPERT, None),
            P(),
        ),
        out_specs=(P(ALL, None), P(ALL, None)),
        check_vma=False,
    )
```

```python
import jax
import jax.numpy as jnp
from jax import lax
from jax.sharding import Mesh, PartitionSpec as P

MAXB = 2
TENSOR = ("tz", "ty")
EXPERT = ("ex", "ec")
ALL = ("ex", "ec", "tz", "ty")
Z_SHARE = 10


norm_eps = 1e-06


def rms_norm(values, gain):
    scale = lax.rsqrt(jnp.mean(values * values, axis=-1, keepdims=True) + norm_eps)
    return values * scale * gain.astype(values.dtype)


def pair_gates(scores):
    first = jax.nn.sigmoid(scores[:, 0] - scores[:, 1])
    return jnp.stack([first, 1.0 - first], axis=1)


def per_device(
    resid,
    contexts,
    att_routes,
    att_scores,
    att_out_w,
    norm_gain,
    router_w,
    mlp_routes,
    split_rule,
    placement,
    cap_blocks,
    w_gate_up,
    w_down,
    final_gain,
):
    n_tensor = lax.axis_size(TENSOR)
    row_count = resid.shape[0]
    model_width = resid.shape[1]
    group_rows = contexts.shape[0]
    att_experts = att_out_w.shape[0]
    slice_ctx = att_out_w.shape[1]
    top_count = att_routes.shape[1]
    gate_att = pair_gates(att_scores)
    width = att_experts * slice_ctx
    column = jnp.arange(width, dtype=jnp.int32)
    source = jnp.arange(slice_ctx * top_count, dtype=jnp.int32)[:, None]
    mixed = jnp.zeros((group_rows, width), jnp.float32)
    for choice in range(top_count):
        spread = (source == (column % slice_ctx)[None, :] * top_count + choice).astype(jnp.bfloat16)
        picked = jnp.dot(contexts, spread, preferred_element_type=jnp.float32)
        chosen = att_routes[:, choice : choice + 1] == (column // slice_ctx)[None, :]
        mixed = mixed + jnp.where(chosen, picked * gate_att[:, choice : choice + 1], 0.0)
    row_block = mixed.astype(jnp.bfloat16)
    weight_flat = att_out_w.reshape(width, model_width)
    n_y = lax.axis_size("ty")
    n_z = lax.axis_size("tz")
    split = model_width * Z_SHARE // 16
    z_first = jnp.dot(row_block, weight_flat[:, :split], preferred_element_type=jnp.float32)
    z_first = lax.psum_scatter(z_first.astype(jnp.bfloat16), "tz", scatter_dimension=0, tiled=True)
    z_first = lax.psum_scatter(z_first, "ty", scatter_dimension=0, tiled=True).astype(jnp.float32)
    by_y = row_block.reshape(n_z, n_y, -1, width).transpose(1, 0, 2, 3).reshape(group_rows, width)
    y_first = jnp.dot(by_y, weight_flat[:, split:], preferred_element_type=jnp.float32)
    y_first = lax.all_to_all(y_first.astype(jnp.bfloat16), "ty", split_axis=0, concat_axis=0, tiled=True)
    y_first = jnp.sum(y_first.reshape(n_y, -1, model_width - split).astype(jnp.float32), axis=0)
    y_first = lax.all_to_all(y_first.astype(jnp.bfloat16), "tz", split_axis=0, concat_axis=0, tiled=True)
    y_first = jnp.sum(y_first.reshape(n_z, -1, model_width - split).astype(jnp.float32), axis=0)
    attention = jnp.concatenate([z_first, y_first], axis=1)
    stream = (resid.astype(jnp.float32) + attention).astype(jnp.bfloat16)
    normed = rms_norm(stream.astype(jnp.float32), norm_gain).astype(jnp.bfloat16)
    logits = jnp.dot(normed, router_w, preferred_element_type=jnp.float32)
    gate_mlp = pair_gates(jnp.take_along_axis(logits, mlp_routes, axis=1))
    replicas = placement.shape[0]
    slots = w_gate_up.shape[0]
    expert_total = router_w.shape[1]
    block_rows = max(1, row_count * top_count // (2 * replicas))
    capacity_rows = MAXB * block_rows
    slot_ids = jnp.arange(replicas, dtype=jnp.int32)
    expert_ids = jnp.arange(expert_total, dtype=jnp.int32)
    copies = jnp.sum((placement[None, :] == expert_ids[:, None]).astype(jnp.int32), axis=1)
    earlier = jnp.sum(
        (
            (placement[None, :] == placement[:, None]) & (slot_ids[None, :] < slot_ids[:, None])
        ).astype(jnp.int32),
        axis=1,
    )
    route_onehot = (mlp_routes[:, :, None] == expert_ids[None, None, :]).astype(jnp.int32)
    route_copies = jnp.sum(route_onehot * copies[None, None, :], axis=2)
    replica_rank = jnp.remainder(split_rule, route_copies)
    match = (
        (placement[None, None, :] == mlp_routes[:, :, None])
        & (earlier[None, None, :] == replica_rank[:, :, None])
    ).astype(jnp.int32)
    replica_slot = jnp.sum(match * slot_ids[None, None, :], axis=2)
    capacity = jnp.sum(match * cap_blocks[None, None, :], axis=2) * block_rows
    flat_match = match.reshape(row_count * top_count, replicas)
    before = jnp.cumsum(flat_match, axis=0) - flat_match
    arrival = jnp.sum(before * flat_match, axis=1).reshape(row_count, top_count)
    is_kept = arrival < capacity
    holder = replica_slot // slots
    within = replica_slot % slots
    position = within * (n_tensor * capacity_rows) + holder * capacity_rows + arrival
    position = jnp.where(is_kept, position, -1)
    buffer_rows = slots * n_tensor * capacity_rows
    placer = jnp.sum(
        (jnp.arange(buffer_rows, dtype=jnp.int32)[:, None, None] == position[None, :, :]).astype(
            jnp.bfloat16
        ),
        axis=2,
    )
    send_rows = jnp.dot(placer, normed, preferred_element_type=jnp.float32).astype(jnp.bfloat16)
    exchanged = lax.all_to_all(send_rows, TENSOR, split_axis=0, concat_axis=0, tiled=True)
    arrived = lax.all_gather(exchanged, "ex", axis=0, tiled=True)
    swap = [(0, 1), (1, 0)]
    paired_gate_up = lax.ppermute(w_gate_up, "ec", swap)
    paired_down = lax.ppermute(w_down, "ec", swap)
    hidden_units = w_gate_up.shape[3]

    def expert_part(gate_up, down_w):
        both = jnp.dot(
            arrived, gate_up.reshape(model_width, 2 * hidden_units), preferred_element_type=jnp.float32
        )
        hidden = (jax.nn.silu(both[:, :hidden_units]) * both[:, hidden_units:]).astype(jnp.bfloat16)
        return jnp.dot(
            hidden, down_w.reshape(hidden_units, model_width), preferred_element_type=jnp.float32
        )

    down = expert_part(w_gate_up, w_down) + expert_part(paired_gate_up, paired_down)
    summed = lax.psum_scatter(down.astype(jnp.bfloat16), "ex", scatter_dimension=0, tiled=True)
    flat_back = lax.all_to_all(summed, TENSOR, split_axis=0, concat_axis=0, tiled=True)
    back_index = jnp.where(is_kept, holder * (capacity_rows * slots) + arrival * slots + within, 0)
    factors = gate_mlp * is_kept.astype(jnp.float32)
    back_rows = flat_back.shape[0]
    select = jnp.sum(
        jnp.where(
            back_index[:, :, None] == jnp.arange(back_rows, dtype=jnp.int32)[None, None, :],
            factors[:, :, None],
            0.0,
        ),
        axis=1,
    )
    expert_mix = jnp.dot(
        select, flat_back.astype(jnp.float32), precision=lax.Precision.HIGHEST,
        preferred_element_type=jnp.float32,
    )
    after = stream.astype(jnp.float32) + expert_mix
    return (after.astype(jnp.bfloat16), rms_norm(after, final_gain).astype(jnp.bfloat16))


def split_mesh(mesh):
    n_expert, n_tensor = mesh.devices.shape
    n_y = 4 if n_tensor % 4 == 0 else 1
    shape = (n_expert // 2, 2, n_tensor // n_y, n_y)
    return Mesh(mesh.devices.reshape(shape), ALL)


def solution(mesh):
    mesh = split_mesh(mesh)
    return jax.shard_map(
        per_device,
        mesh=mesh,
        in_specs=(
            P(ALL, None),
            P(EXPERT, TENSOR),
            P(EXPERT, None),
            P(EXPERT, None),
            P(None, TENSOR, None),
            P(),
            P(),
            P(ALL, None),
            P(ALL, None),
            P(),
            P(),
            P(TENSOR, None, None, EXPERT),
            P(TENSOR, EXPERT, None),
            P(),
        ),
        out_specs=(P(ALL, None), P(ALL, None)),
        check_vma=False,
    )
```
